512 devices in a mesh: dp: 64 (over z, x_lo, core), slab: 8 (over y, x_hi).
Axes of the slice: x: 4 (x_hi: 2, x_lo: 2; x = x_hi * 2 + x_lo), y: 4, z: 16, core: 2. Of those that a mesh axis runs over, the one named last changes fastest.
Arguments:
- voxels: bfloat16 [64, 8, 12, 32, 128], P('dp', None, None, 'slab'), may hold values from -16 to 16
- occupancy: int32 [64, 8, 12, 32], P('dp', None, None, 'slab'), may hold values 0 or 1
- out_grad: bfloat16 [64, 8, 12, 32, 128], P('dp', None, None, 'slab'), may hold values from -192 to 192
- weights: bfloat16 [2, 3456, 128], replicated, may hold values from -5 to 5
- master: float32 [2, 3456, 128], P(None, 'dp', 'slab'), may hold values from -5 to 5
- moment: float32 [2, 3456, 128], P(None, 'dp', 'slab'), may hold values from -18 to 18
- second: float32 [2, 3456, 128], P(None, 'dp', 'slab'), may hold values from 1 to 10
- teacher: float32 [2, 3456, 128], P(None, 'dp', 'slab'), may hold values from -5 to 5
Outputs:
- new_master: float32 [2, 3456, 128], P(None, 'dp', 'slab')
- new_moment: float32 [2, 3456, 128], P(None, 'dp', 'slab')
- new_second: float32 [2, 3456, 128], P(None, 'dp', 'slab')
- new_teacher: float32 [2, 3456, 128], P(None, 'dp', 'slab')
- new_weights: bfloat16 [2, 3456, 128], P(None, None, 'slab')
The draws below stay inside these ranges and needn't reach their ends.
All inputs are finite; a program needn't handle non-finite values. No bound on the sum of `occupancy` on one device may be relied on, other than what follows from the above.
Results may differ from the reference program's by a relative error of at most 0.0013.
Values may be sent and summed in bfloat16 or wider, within the bound.
No kernel may reach another device: no remote copies, remote signals or barrier semaphores. Data moves between devices by JAX's collectives and lax.ppermute only.
A program may use at most 64 MiB of HBM per device.

```python
import math
import jax
import jax.numpy as jnp
from jax import lax

C = 128
TAPS = 27
LAYERS = 2
STEP_COUNT = 10
WX = 8
WY = 12
KC = 3456
GZ = 32
SCENES = 64


def set_ends(array, key, smallest, largest):
    shape = array.shape
    spot = [jax.random.randint(jax.random.fold_in(key, axis), (), 0, shape[axis]) for axis in range(len(shape))]
    array = array.at[tuple(spot)].set(smallest)
    longest = shape.index(max(shape))
    spot[longest] = (spot[longest] + 1) % shape[longest]
    return array.at[tuple(spot)].set(largest)


def with_spikes(array, rng, source, target, shards_of, factor):
    def block_of(axis_at):
        return (jnp.arange(array.shape[axis_at]) // (array.shape[axis_at] // shards_of)).reshape((-1,) + (1,) * (array.ndim - 1 - axis_at))

    one_side = jax.random.permutation(rng, shards_of)[block_of(target)]
    second = (block_of(target) + shards_of // 2) % shards_of
    return jnp.where((block_of(source) == one_side) | (block_of(source) == second), factor * array, array)


def levels(key, dims, shards, low, high):
    gain, own = 1.0, jax.random.fold_in(key, 6)
    for position, blocks in shards:
        draws = jnp.exp(jax.random.uniform(jax.random.fold_in(own, position), (blocks,), jnp.float32, low / len(shards), high / len(shards)))
        gain = gain * jnp.repeat(draws, dims[position] // blocks).reshape([-1 if axis == position else 1 for axis in range(len(dims))])
    return gain


def bell_draw(key, shape, spread, bound, pieces=(), kind=jnp.bfloat16):
    result = spread * jax.random.normal(key, shape, jnp.float32)
    if pieces:
        result = result * levels(key, shape, pieces, -0.22, 0.18)
    return jnp.clip(result, -bound, bound).astype(kind)


def noise_with(own_key, dims, deviation, most, pieces, heavy, kind=jnp.bfloat16):
    values = deviation * jax.random.normal(own_key, dims, jnp.float32)
    if pieces:
        values = values * levels(own_key, dims, pieces, -0.22, 0.18)
    return jnp.clip(with_spikes(values, jax.random.fold_in(own_key, 3), *heavy), -most, most).astype(kind)


def setup_inputs(seed: int = 0) -> dict:
    key_of = jax.random.split(jax.random.key(seed), 9)
    return {
        "voxels": noise_with(key_of[0], (SCENES, WX, WY, GZ, C), 1.0, 16.0, ((0, 64), (3, 8)), (0, 4, 64, 4.0)),
        "occupancy": set_ends((jax.random.randint(key_of[1], (SCENES, WX, WY, GZ), 0, 2) < 1).astype(jnp.int32), jax.random.fold_in(key_of[1], 1), 0, 1),
        "out_grad": bell_draw(key_of[2], (SCENES, WX, WY, GZ, C), 32.0, 192.0, ((0, 64), (3, 8))),
        "weights": bell_draw(key_of[3], (LAYERS, KC, C), 1.0, 5.0),
        "master": bell_draw(key_of[4], (LAYERS, KC, C), 0.5, 5.0, ((1, 64), (2, 8)), jnp.float32),
        "moment": bell_draw(key_of[5], (LAYERS, KC, C), 3.0, 18.0, ((1, 64), (2, 8)), jnp.float32),
        "second": jnp.clip(jnp.exp(math.log(10.0) - 2.3025851 * jax.random.uniform(key_of[6], (LAYERS, KC, C), jnp.float32) ** levels(key_of[6], (LAYERS, KC, C), ((1, 64), (2, 8)), -0.2, 0.2)), 1.0, 10.0),
        "teacher": bell_draw(key_of[7], (LAYERS, KC, C), 1.0, 5.0, ((1, 64), (2, 8)), jnp.float32),
    }


beta_first = 0.9
beta_second = 0.999
learning_rate = 0.01
weight_decay = 0.05
teacher_keep = 0.99
adam_epsilon = 1e-08

def tap_corners():
    return [(along_x, along_y, along_z) for along_x in range(3) for along_y in range(3) for along_z in range(3)]

def unit_scale():
    return (TAPS * C) ** (-0.5)

def silu_slope(values):
    logistic = jax.nn.sigmoid(values)
    return logistic * (1.0 + values * (1.0 - logistic))

def forward_conv(padded, weight_rows, extent):
    summed = jnp.zeros(extent + (C,), jnp.float32)
    for tap_index, corner in enumerate(tap_corners()):
        window = padded[corner[0]:corner[0] + extent[0], corner[1]:corner[1] + extent[1], corner[2]:corner[2] + extent[2]]
        block = weight_rows[tap_index * C:(tap_index + 1) * C]
        summed = summed + jnp.einsum('xyzi,io->xyzo', window, block, precision=lax.Precision.HIGHEST)
    return summed * unit_scale()

def transposed_conv(padded_grad, weight_rows, extent):
    summed = jnp.zeros(extent + (C,), jnp.float32)
    for tap_index, corner in enumerate(tap_corners()):
        window = padded_grad[2 - corner[0]:2 - corner[0] + extent[0], 2 - corner[1]:2 - corner[1] + extent[1], 2 - corner[2]:2 - corner[2] + extent[2]]
        block = weight_rows[tap_index * C:(tap_index + 1) * C]
        summed = summed + jnp.einsum('xyzo,io->xyzi', window, block, precision=lax.Precision.HIGHEST)
    return summed * unit_scale()

def weight_grad(padded, grad_field, extent):
    blocks = []
    for corner in tap_corners():
        window = padded[corner[0]:corner[0] + extent[0], corner[1]:corner[1] + extent[1], corner[2]:corner[2] + extent[2]]
        blocks.append(jnp.einsum('xyzi,xyzo->io', window, grad_field, precision=lax.Precision.HIGHEST))
    return jnp.concatenate(blocks, axis=0) * unit_scale()

def scene_terms(weights_float, scene_voxels, occupy, cotangent):
    extent = tuple(scene_voxels.shape[:3])
    occupied = occupy.astype(jnp.float32)[..., None]
    padding = ((1, 1), (1, 1), (1, 1), (0, 0))
    padded_in = jnp.pad(scene_voxels.astype(jnp.float32), padding)
    pre_one = forward_conv(padded_in, weights_float[0], extent)
    act_one = (occupied * jax.nn.silu(pre_one)).astype(jnp.bfloat16)
    padded_act = jnp.pad(act_one.astype(jnp.float32), padding)
    pre_two = forward_conv(padded_act, weights_float[1], extent)
    grad_two = (cotangent.astype(jnp.float32) * occupied * silu_slope(pre_two)).astype(jnp.bfloat16)
    grad_float = grad_two.astype(jnp.float32)
    padded_grad = jnp.pad(grad_float, padding)
    wgrad_two = weight_grad(padded_act, grad_float, extent)
    back_one = transposed_conv(padded_grad, weights_float[1], extent)
    grad_one = (back_one * occupied * silu_slope(pre_one)).astype(jnp.bfloat16)
    wgrad_one = weight_grad(padded_in, grad_one.astype(jnp.float32), extent)
    return jnp.stack([wgrad_one, wgrad_two])

def adam_update(master, moment, second, teacher, gradient):
    new_moment = beta_first * moment + (1.0 - beta_first) * gradient
    new_second = beta_second * second + (1.0 - beta_second) * gradient * gradient
    first_fix = 1.0 - beta_first ** STEP_COUNT
    second_fix = 1.0 - beta_second ** STEP_COUNT
    ratio = new_moment / first_fix / (jnp.sqrt(new_second / second_fix) + adam_epsilon)
    new_master = master - learning_rate * (ratio + weight_decay * master)
    new_teacher = teacher_keep * teacher + (1.0 - teacher_keep) * new_master
    return (new_master, new_moment, new_second, new_teacher)

def reference(voxels, occupancy, out_grad, weights, master, moment, second, teacher):
    weights_float = weights.astype(jnp.float32)

    def accumulate(running, inputs):
        scene_voxels, occupy, cotangent = inputs
        return (running + scene_terms(weights_float, scene_voxels, occupy, cotangent), None)
    gradient, unused = lax.scan(accumulate, jnp.zeros(weights.shape, jnp.float32), (voxels, occupancy, out_grad))
    new_master, new_moment, new_second, new_teacher = adam_update(master, moment, second, teacher, gradient)
    return (new_master, new_moment, new_second, new_teacher, new_master.astype(jnp.bfloat16))
```

```python
import jax
import jax.numpy as jnp
from jax import lax
from jax.sharding import PartitionSpec as P

C = 128
TAPS = 27
STEP_COUNT = 10


beta_first = 0.9
beta_second = 0.999
learning_rate = 0.01
weight_decay = 0.05
teacher_keep = 0.99
adam_epsilon = 1e-08


def with_halo(cells, sides, width):
    for axis, dim in sides:
        count = lax.axis_size(axis)
        ends = count - 1
        head = lax.slice_in_dim(cells, 0, width, axis=dim)
        tail = lax.slice_in_dim(cells, cells.shape[dim] - width, cells.shape[dim], axis=dim)
        cells = jnp.concatenate(
            [
                lax.ppermute(tail, axis, [(i, (i + 1) % count) for i in range(ends)]),
                cells,
                lax.ppermute(head, axis, [((i + 1) % count, i) for i in range(ends)]),
            ],
            axis=dim,
        )
    return cells


def tap_corners():
    return [
        (along_x, along_y, along_z)
        for along_x in range(3)
        for along_y in range(3)
        for along_z in range(3)
    ]


def unit_scale():
    return (TAPS * C) ** (-0.5)


def silu_slope(values):
    logistic = jax.nn.sigmoid(values)
    return logistic * (1.0 + values * (1.0 - logistic))


def take_window(padded, start, extent):
    window = padded[
        start[0] : start[0] + extent[0],
        start[1] : start[1] + extent[1],
        start[2] : start[2] + extent[2],
    ]
    return window.reshape(-1, window.shape[-1])


def forward_conv(padded, weight_rows, extent):
    channels = weight_rows.shape[1]
    summed = jnp.zeros((extent[0] * extent[1] * extent[2], channels), jnp.float32)
    for tap_index, corner in enumerate(tap_corners()):
        window = take_window(padded, corner, extent)
        block = weight_rows[tap_index * channels : (tap_index + 1) * channels]
        summed = summed + jnp.dot(window, block, preferred_element_type=jnp.float32)
    return (summed * unit_scale()).reshape(extent + (channels,))


def transposed_conv(padded_grad, weight_rows, extent):
    channels = weight_rows.shape[1]
    summed = jnp.zeros((extent[0] * extent[1] * extent[2], channels), jnp.float32)
    for tap_index, corner in enumerate(tap_corners()):
        start = (2 - corner[0], 2 - corner[1], 2 - corner[2])
        window = take_window(padded_grad, start, extent)
        block = weight_rows[tap_index * channels : (tap_index + 1) * channels]
        summed = summed + lax.dot_general(
            window, block, (((1,), (1,)), ((), ())), preferred_element_type=jnp.float32
        )
    return (summed * unit_scale()).reshape(extent + (channels,))


def weight_grad(padded, grad_field, extent):
    grad_rows = grad_field.reshape(-1, grad_field.shape[-1])
    blocks = []
    for corner in tap_corners():
        window = take_window(padded, corner, extent)
        blocks.append(
            lax.dot_general(
                window, grad_rows, (((0,), (0,)), ((), ())), preferred_element_type=jnp.float32
            )
        )
    return jnp.concatenate(blocks, axis=0) * unit_scale()


def adam_update(master, moment, second, teacher, gradient):
    new_moment = beta_first * moment + (1.0 - beta_first) * gradient
    new_second = beta_second * second + (1.0 - beta_second) * gradient * gradient
    first_fix = 1.0 - beta_first**STEP_COUNT
    second_fix = 1.0 - beta_second**STEP_COUNT
    ratio = new_moment / first_fix / (jnp.sqrt(new_second / second_fix) + adam_epsilon)
    new_master = master - learning_rate * (ratio + weight_decay * master)
    new_teacher = teacher_keep * teacher + (1.0 - teacher_keep) * new_master
    return (new_master, new_moment, new_second, new_teacher)


def local(voxels, occupancy, out_grad, weights, master, moment, second, teacher):
    own_cells = voxels[0]
    extent = tuple(own_cells.shape[:3])
    occupied = occupancy[0].astype(jnp.float32)[..., None]
    plane_pad = ((1, 1), (1, 1), (0, 0), (0, 0))
    rim_input = with_halo(own_cells, ((COLUMN_AXES, 2),), 1)
    padded_in = jnp.pad(rim_input, plane_pad)
    pre_one = forward_conv(padded_in, weights[0], extent)
    act_one = (occupied * jax.nn.silu(pre_one)).astype(jnp.bfloat16)
    rim_hidden = with_halo(act_one, ((COLUMN_AXES, 2),), 1)
    padded_act = jnp.pad(rim_hidden, plane_pad)
    pre_two = forward_conv(padded_act, weights[1], extent)
    grad_two = (out_grad[0].astype(jnp.float32) * occupied * silu_slope(pre_two)).astype(
        jnp.bfloat16
    )
    rim_grad = with_halo(grad_two, ((COLUMN_AXES, 2),), 1)
    padded_grad = jnp.pad(rim_grad, plane_pad)
    wgrad_two = weight_grad(padded_act, grad_two, extent)
    back_one = transposed_conv(padded_grad, weights[1], extent)
    grad_one = (back_one * occupied * silu_slope(pre_one)).astype(jnp.bfloat16)
    wgrad_one = weight_grad(padded_in, grad_one, extent)
    weight_grads = jnp.stack([wgrad_one, wgrad_two])
    gradient = scatter_rows_and_columns(weight_grads, master.shape)
    new_master, new_moment, new_second, new_teacher = adam_update(
        master, moment, second, teacher, gradient
    )
    fresh_weights = new_master.astype(jnp.bfloat16)
    new_weights = gather_rows(fresh_weights)
    return (new_master, new_moment, new_second, new_teacher, new_weights)


ROW_AXES = ("z", "x_lo", "core")
COLUMN_AXES = ("y", "x_hi")


def scatter_rows_and_columns(weight_grads, own_shape):
    layers, rows, cols = own_shape
    z, x_lo, core = (lax.axis_size(name) for name in ROW_AXES)
    y, x_hi = (lax.axis_size(name) for name in COLUMN_AXES)
    blocks = weight_grads.reshape(layers, z, x_lo, core, rows, y, x_hi, cols)
    blocks = blocks.transpose(3, 5, 6, 2, 1, 0, 4, 7)
    blocks = lax.psum_scatter(blocks, "core", scatter_dimension=0, tiled=True)[0]
    blocks = lax.psum_scatter(blocks, "y", scatter_dimension=0, tiled=True)[0]
    blocks = blocks.reshape((x_hi * x_lo,) + blocks.shape[2:])
    blocks = lax.psum_scatter(blocks, ("x_hi", "x_lo"), scatter_dimension=0, tiled=True)[0]
    blocks = lax.psum_scatter(blocks, "z", scatter_dimension=0, tiled=True)[0]
    return blocks


def gather_rows(fresh_weights):
    layers, rows, cols = fresh_weights.shape
    gathered = lax.all_gather(fresh_weights, "z", axis=0)
    gathered = lax.all_gather(gathered, ("x_lo", "core"), axis=0)
    gathered = gathered.reshape((-1,) + gathered.shape[1:])
    x_lo, core = lax.axis_size("x_lo"), lax.axis_size("core")
    gathered = gathered.reshape((x_lo, core) + gathered.shape[1:])
    gathered = gathered.transpose(3, 2, 0, 1, 4, 5)
    return gathered.reshape(layers, -1, cols)


def solution(mesh):
    rows_over, columns_over = mesh.shape["dp"], mesh.shape["slab"]
    fine = jax.sharding.Mesh(
        mesh.devices.reshape(rows_over // 4, 2, 2, columns_over // 2, 2), ROW_AXES + COLUMN_AXES
    )
    dp, slab = ROW_AXES, COLUMN_AXES
    in_specs = (
        P(dp, None, None, slab, None),
        P(dp, None, None, slab),
        P(dp, None, None, slab, None),
        P(),
        P(None, dp, slab),
        P(None, dp, slab),
        P(None, dp, slab),
        P(None, dp, slab),
    )
    out_specs = (
        P(None, dp, slab),
        P(None, dp, slab),
        P(None, dp, slab),
        P(None, dp, slab),
        P(None, None, slab),
    )
    return jax.shard_map(local, mesh=fine, in_specs=in_specs, out_specs=out_specs, check_vma=False)
```

```python
import jax
import jax.numpy as jnp
from jax import lax
from jax.sharding import PartitionSpec as P

C = 128
TAPS = 27
STEP_COUNT = 10


beta_first = 0.9
beta_second = 0.999
learning_rate = 0.01
weight_decay = 0.05
teacher_keep = 0.99
adam_epsilon = 1e-08


def with_halo(cells, sides, width):
    for axis, dim in sides:
        count = lax.axis_size(axis)
        ends = count - 1
        head = lax.slice_in_dim(cells, 0, width, axis=dim)
        tail = lax.slice_in_dim(cells, cells.shape[dim] - width, cells.shape[dim], axis=dim)
        cells = jnp.concatenate(
            [
                lax.ppermute(tail, axis, [(i, (i + 1) % count) for i in range(ends)]),
                cells,
                lax.ppermute(head, axis, [((i + 1) % count, i) for i in range(ends)]),
            ],
            axis=dim,
        )
    return cells


def tap_corners():
    return [
        (along_x, along_y, along_z)
        for along_x in range(3)
        for along_y in range(3)
        for along_z in range(3)
    ]


def unit_scale():
    return (TAPS * C) ** (-0.5)


def silu_slope(values):
    logistic = jax.nn.sigmoid(values)
    return logistic * (1.0 + values * (1.0 - logistic))


def take_window(padded, start, extent):
    window = padded[
        start[0] : start[0] + extent[0],
        start[1] : start[1] + extent[1],
        start[2] : start[2] + extent[2],
    ]
    return window.reshape(-1, window.shape[-1])


def forward_conv(padded, weight_rows, extent):
    channels = weight_rows.shape[1]
    summed = jnp.zeros((extent[0] * extent[1] * extent[2], channels), jnp.float32)
    for tap_index, corner in enumerate(tap_corners()):
        window = take_window(padded, corner, extent)
        block = weight_rows[tap_index * channels : (tap_index + 1) * channels]
        summed = summed + jnp.dot(window, block, preferred_element_type=jnp.float32)
    return (summed * unit_scale()).reshape(extent + (channels,))


def transposed_conv(padded_grad, weight_rows, extent):
    channels = weight_rows.shape[1]
    summed = jnp.zeros((extent[0] * extent[1] * extent[2], channels), jnp.float32)
    for tap_index, corner in enumerate(tap_corners()):
        start = (2 - corner[0], 2 - corner[1], 2 - corner[2])
        window = take_window(padded_grad, start, extent)
        block = weight_rows[tap_index * channels : (tap_index + 1) * channels]
        summed = summed + lax.dot_general(
            window, block, (((1,), (1,)), ((), ())), preferred_element_type=jnp.float32
        )
    return (summed * unit_scale()).reshape(extent + (channels,))


def weight_grad(padded, grad_field, extent):
    grad_rows = grad_field.reshape(-1, grad_field.shape[-1])
    blocks = []
    for corner in tap_corners():
        window = take_window(padded, corner, extent)
        blocks.append(
            lax.dot_general(
                window, grad_rows, (((0,), (0,)), ((), ())), preferred_element_type=jnp.float32
            )
        )
    return jnp.concatenate(blocks, axis=0) * unit_scale()


def adam_update(master, moment, second, teacher, gradient):
    new_moment = beta_first * moment + (1.0 - beta_first) * gradient
    new_second = beta_second * second + (1.0 - beta_second) * gradient * gradient
    first_fix = 1.0 - beta_first**STEP_COUNT
    second_fix = 1.0 - beta_second**STEP_COUNT
    ratio = new_moment / first_fix / (jnp.sqrt(new_second / second_fix) + adam_epsilon)
    new_master = master - learning_rate * (ratio + weight_decay * master)
    new_teacher = teacher_keep * teacher + (1.0 - teacher_keep) * new_master
    return (new_master, new_moment, new_second, new_teacher)


def local(voxels, occupancy, out_grad, weights, master, moment, second, teacher):
    own_cells = voxels[0]
    extent = tuple(own_cells.shape[:3])
    occupied = occupancy[0].astype(jnp.float32)[..., None]
    plane_pad = ((1, 1), (1, 1), (0, 0), (0, 0))
    rim_input = with_halo(own_cells, ((COLUMN_AXES, 2),), 1)
    padded_in = jnp.pad(rim_input, plane_pad)
    pre_one = forward_conv(padded_in, weights[0], extent)
    act_one = (occupied * jax.nn.silu(pre_one)).astype(jnp.bfloat16)
    rim_hidden = with_halo(act_one, ((COLUMN_AXES, 2),), 1)
    padded_act = jnp.pad(rim_hidden, plane_pad)
    pre_two = forward_conv(padded_act, weights[1], extent)
    grad_two = (out_grad[0].astype(jnp.float32) * occupied * silu_slope(pre_two)).astype(
        jnp.bfloat16
    )
    rim_grad = with_halo(grad_two, ((COLUMN_AXES, 2),), 1)
    padded_grad = jnp.pad(rim_grad, plane_pad)
    wgrad_two = weight_grad(padded_act, grad_two, extent)
    back_one = transposed_conv(padded_grad, weights[1], extent)
    grad_one = (back_one * occupied * silu_slope(pre_one)).astype(jnp.bfloat16)
    wgrad_one = weight_grad(padded_in, grad_one, extent)
    weight_grads = jnp.stack([wgrad_one, wgrad_two])
    gradient = scatter_rows_and_columns(weight_grads, master.shape)
    new_master, new_moment, new_second, new_teacher = adam_update(
        master, moment, second, teacher, gradient
    )
    fresh_weights = new_master.astype(jnp.bfloat16)
    new_weights = gather_rows(fresh_weights)
    return (new_master, new_moment, new_second, new_teacher, new_weights)


ROW_AXES = ("z", "x_lo", "core")
COLUMN_AXES = ("y", "x_hi")


def exchange_and_sum(blocks, axes):
    moved = lax.all_to_all(blocks, axes, 0, 0, tiled=True)
    return moved.sum(axis=0)


def scatter_rows_and_columns(weight_grads, own_shape):
    layers, rows, cols = own_shape
    z, x_lo, core = (lax.axis_size(name) for name in ROW_AXES)
    y, x_hi = (lax.axis_size(name) for name in COLUMN_AXES)
    blocks = weight_grads.reshape(layers, z, x_lo, core, rows, y, x_hi, cols)
    blocks = blocks.transpose(3, 5, 6, 2, 1, 0, 4, 7)
    blocks = exchange_and_sum(blocks, "core")
    blocks = exchange_and_sum(blocks, "y")
    blocks = blocks.reshape((x_hi * x_lo,) + blocks.shape[2:])
    blocks = exchange_and_sum(blocks, ("x_hi", "x_lo"))
    return exchange_and_sum(blocks, "z")


def gather_rows(fresh_weights):
    layers, rows, cols = fresh_weights.shape
    gathered = lax.all_gather(fresh_weights, "z", axis=0)
    gathered = lax.all_gather(gathered, ("x_lo", "core"), axis=0)
    gathered = gathered.reshape((-1,) + gathered.shape[1:])
    x_lo, core = lax.axis_size("x_lo"), lax.axis_size("core")
    gathered = gathered.reshape((x_lo, core) + gathered.shape[1:])
    gathered = gathered.transpose(3, 2, 0, 1, 4, 5)
    return gathered.reshape(layers, -1, cols)


def solution(mesh):
    rows_over, columns_over = mesh.shape["dp"], mesh.shape["slab"]
    fine = jax.sharding.Mesh(
        mesh.devices.reshape(rows_over // 4, 2, 2, columns_over // 2, 2), ROW_AXES + COLUMN_AXES
    )
    dp, slab = ROW_AXES, COLUMN_AXES
    in_specs = (
        P(dp, None, None, slab, None),
        P(dp, None, None, slab),
        P(dp, None, None, slab, None),
        P(),
        P(None, dp, slab),
        P(None, dp, slab),
        P(None, dp, slab),
        P(None, dp, slab),
    )
    out_specs = (
        P(None, dp, slab),
        P(None, dp, slab),
        P(None, dp, slab),
        P(None, dp, slab),
        P(None, None, slab),
    )
    return jax.shard_map(local, mesh=fine, in_specs=in_specs, out_specs=out_specs, check_vma=False)
```

```python
import jax
import jax.numpy as jnp
from jax import lax
from jax.sharding import PartitionSpec as P

C = 128
TAPS = 27
STEP_COUNT = 10


beta_first = 0.9
beta_second = 0.999
learning_rate = 0.01
weight_decay = 0.05
teacher_keep = 0.99
adam_epsilon = 1e-08


def with_halo(cells, sides, width):
    for axis, dim in sides:
        count = lax.axis_size(axis)
        ends = count - 1
        head = lax.slice_in_dim(cells, 0, width, axis=dim)
        tail = lax.slice_in_dim(cells, cells.shape[dim] - width, cells.shape[dim], axis=dim)
        cells = jnp.concatenate(
            [
                lax.ppermute(tail, axis, [(i, (i + 1) % count) for i in range(ends)]),
                cells,
                lax.ppermute(head, axis, [((i + 1) % count, i) for i in range(ends)]),
            ],
            axis=dim,
        )
    return cells


def tap_corners():
    return [
        (along_x, along_y, along_z)
        for along_x in range(3)
        for along_y in range(3)
        for along_z in range(3)
    ]


def unit_scale():
    return (TAPS * C) ** (-0.5)


def silu_slope(values):
    logistic = jax.nn.sigmoid(values)
    return logistic * (1.0 + values * (1.0 - logistic))


def take_window(padded, start, extent):
    window = padded[
        start[0] : start[0] + extent[0],
        start[1] : start[1] + extent[1],
        start[2] : start[2] + extent[2],
    ]
    return window.reshape(-1, window.shape[-1])


def forward_conv(padded, weight_rows, extent):
    channels = weight_rows.shape[1]
    summed = jnp.zeros((extent[0] * extent[1] * extent[2], channels), jnp.float32)
    for tap_index, corner in enumerate(tap_corners()):
        window = take_window(padded, corner, extent)
        block = weight_rows[tap_index * channels : (tap_index + 1) * channels]
        summed = summed + jnp.dot(window, block, preferred_element_type=jnp.float32)
    return (summed * unit_scale()).reshape(extent + (channels,))


def transposed_conv(padded_grad, weight_rows, extent):
    channels = weight_rows.shape[1]
    summed = jnp.zeros((extent[0] * extent[1] * extent[2], channels), jnp.float32)
    for tap_index, corner in enumerate(tap_corners()):
        start = (2 - corner[0], 2 - corner[1], 2 - corner[2])
        window = take_window(padded_grad, start, extent)
        block = weight_rows[tap_index * channels : (tap_index + 1) * channels]
        summed = summed + lax.dot_general(
            window, block, (((1,), (1,)), ((), ())), preferred_element_type=jnp.float32
        )
    return (summed * unit_scale()).reshape(extent + (channels,))


def weight_grad(padded, grad_field, extent):
    grad_rows = grad_field.reshape(-1, grad_field.shape[-1])
    blocks = []
    for corner in tap_corners():
        window = take_window(padded, corner, extent)
        blocks.append(
            lax.dot_general(
                window, grad_rows, (((0,), (0,)), ((), ())), preferred_element_type=jnp.float32
            )
        )
    return jnp.concatenate(blocks, axis=0)


def adam_update(master, moment, second, teacher, gradient):
    new_moment = beta_first * moment + (1.0 - beta_first) * gradient
    new_second = beta_second * second + (1.0 - beta_second) * gradient * gradient
    first_fix = 1.0 - beta_first**STEP_COUNT
    second_fix = 1.0 - beta_second**STEP_COUNT
    ratio = new_moment / first_fix / (jnp.sqrt(new_second / second_fix) + adam_epsilon)
    new_master = master - learning_rate * (ratio + weight_decay * master)
    new_teacher = teacher_keep * teacher + (1.0 - teacher_keep) * new_master
    return (new_master, new_moment, new_second, new_teacher)


def local(voxels, occupancy, out_grad, weights, master, moment, second, teacher):
    own_cells = voxels[0]
    extent = tuple(own_cells.shape[:3])
    occupied = occupancy[0].astype(jnp.float32)[..., None]
    plane_pad = ((1, 1), (1, 1), (0, 0), (0, 0))
    rim_input = with_halo(own_cells, ((COLUMN_AXES, 2),), 1)
    padded_in = jnp.pad(rim_input, plane_pad)
    pre_one = forward_conv(padded_in, weights[0], extent)
    act_one = (occupied * jax.nn.silu(pre_one)).astype(jnp.bfloat16)
    rim_hidden = with_halo(act_one, ((COLUMN_AXES, 2),), 1)
    padded_act = jnp.pad(rim_hidden, plane_pad)
    pre_two = forward_conv(padded_act, weights[1], extent)
    grad_two = (out_grad[0].astype(jnp.float32) * occupied * silu_slope(pre_two)).astype(
        jnp.bfloat16
    )
    rim_grad = with_halo(grad_two, ((COLUMN_AXES, 2),), 1)
    padded_grad = jnp.pad(rim_grad, plane_pad)
    wgrad_two = weight_grad(padded_act, grad_two, extent)
    back_one = transposed_conv(padded_grad, weights[1], extent)
    grad_one = (back_one * occupied * silu_slope(pre_one)).astype(jnp.bfloat16)
    wgrad_one = weight_grad(padded_in, grad_one, extent)
    weight_grads = jnp.stack([wgrad_one, wgrad_two])
    gradient = scatter_rows_and_columns(weight_grads, master.shape)
    new_master, new_moment, new_second, new_teacher = adam_update(
        master, moment, second, teacher, gradient
    )
    fresh_weights = new_master.astype(jnp.bfloat16)
    new_weights = gather_rows(fresh_weights)
    return (new_master, new_moment, new_second, new_teacher, new_weights)


ROW_AXES = ("z", "x_lo", "core")
COLUMN_AXES = ("y", "x_hi")


def exchange_and_sum(blocks, axes):
    moved = lax.all_to_all(blocks, axes, 0, 0, tiled=True)
    return moved.sum(axis=0)


def scatter_rows_and_columns(weight_grads, own_shape):
    layers, rows, cols = own_shape
    lanes = weight_grads.shape[-1]
    z, x_lo, core = (lax.axis_size(name) for name in ROW_AXES)
    y, x_hi = (lax.axis_size(name) for name in COLUMN_AXES)
    blocks = weight_grads.reshape(layers, z, x_lo, core, rows, y, x_hi, cols)
    blocks = blocks.transpose(3, 5, 6, 2, 1, 0, 4, 7)
    blocks = exchange_and_sum(blocks.reshape(core, -1, lanes), "core")
    blocks = exchange_and_sum(blocks.reshape(y, -1, lanes), "y")
    blocks = exchange_and_sum(blocks.reshape(x_hi * x_lo, -1, lanes), ("x_hi", "x_lo"))
    blocks = exchange_and_sum(blocks.reshape(z, -1), "z")
    return blocks.reshape(own_shape) * unit_scale()


def gather_rows(fresh_weights):
    layers, rows, cols = fresh_weights.shape
    gathered = lax.all_gather(fresh_weights, "z", axis=0)
    gathered = lax.all_gather(gathered, ("x_lo", "core"), axis=0)
    gathered = gathered.reshape((-1,) + gathered.shape[1:])
    x_lo, core = lax.axis_size("x_lo"), lax.axis_size("core")
    gathered = gathered.reshape((x_lo, core) + gathered.shape[1:])
    gathered = gathered.transpose(3, 2, 0, 1, 4, 5)
    return gathered.reshape(layers, -1, cols)


def solution(mesh):
    rows_over, columns_over = mesh.shape["dp"], mesh.shape["slab"]
    fine = jax.sharding.Mesh(
        mesh.devices.reshape(rows_over // 4, 2, 2, columns_over // 2, 2), ROW_AXES + COLUMN_AXES
    )
    dp, slab = ROW_AXES, COLUMN_AXES
    in_specs = (
        P(dp, None, None, slab, None),
        P(dp, None, None, slab),
        P(dp, None, None, slab, None),
        P(),
        P(None, dp, slab),
        P(None, dp, slab),
        P(None, dp, slab),
        P(None, dp, slab),
    )
    out_specs = (
        P(None, dp, slab),
        P(None, dp, slab),
        P(None, dp, slab),
        P(None, dp, slab),
        P(None, None, slab),
    )
    return jax.shard_map(local, mesh=fine, in_specs=in_specs, out_specs=out_specs, check_vma=False)
```

```python
import jax
import jax.numpy as jnp
from jax import lax
from jax.sharding import PartitionSpec as P

C = 128
TAPS = 27
STEP_COUNT = 10


beta_first = 0.9
beta_second = 0.999
learning_rate = 0.01
weight_decay = 0.05
teacher_keep = 0.99
adam_epsilon = 1e-08


def with_halo(cells, sides, width):
    for axis, dim in sides:
        count = lax.axis_size(axis)
        ends = count - 1
        head = lax.slice_in_dim(cells, 0, width, axis=dim)
        tail = lax.slice_in_dim(cells, cells.shape[dim] - width, cells.shape[dim], axis=dim)
        cells = jnp.concatenate(
            [
                lax.ppermute(tail, axis, [(i, (i + 1) % count) for i in range(ends)]),
                cells,
                lax.ppermute(head, axis, [((i + 1) % count, i) for i in range(ends)]),
            ],
            axis=dim,
        )
    return cells


def tap_corners():
    return [
        (along_x, along_y, along_z)
        for along_x in range(3)
        for along_y in range(3)
        for along_z in range(3)
    ]


def unit_scale():
    return (TAPS * C) ** (-0.5)


def silu_slope(values):
    logistic = jax.nn.sigmoid(values)
    return logistic * (1.0 + values * (1.0 - logistic))


def take_window(padded, start, extent):
    window = padded[
        start[0] : start[0] + extent[0],
        start[1] : start[1] + extent[1],
        start[2] : start[2] + extent[2],
    ]
    return window.reshape(-1, window.shape[-1])


def forward_conv(padded, weight_rows, extent):
    channels = weight_rows.shape[1]
    summed = jnp.zeros((extent[0] * extent[1] * extent[2], channels), jnp.float32)
    for tap_index, corner in enumerate(tap_corners()):
        window = take_window(padded, corner, extent)
        block = weight_rows[tap_index * channels : (tap_index + 1) * channels]
        summed = summed + jnp.dot(window, block, preferred_element_type=jnp.float32)
    return (summed * unit_scale()).reshape(extent + (channels,))


def transposed_conv(padded_grad, weight_rows, extent):
    channels = weight_rows.shape[1]
    summed = jnp.zeros((extent[0] * extent[1] * extent[2], channels), jnp.float32)
    for tap_index, corner in enumerate(tap_corners()):
        start = (2 - corner[0], 2 - corner[1], 2 - corner[2])
        window = take_window(padded_grad, start, extent)
        block = weight_rows[tap_index * channels : (tap_index + 1) * channels]
        summed = summed + lax.dot_general(
            window, block, (((1,), (1,)), ((), ())), preferred_element_type=jnp.float32
        )
    return (summed * unit_scale()).reshape(extent + (channels,))


def weight_grad(padded, grad_field, extent):
    grad_rows = grad_field.reshape(-1, grad_field.shape[-1])
    blocks = []
    for corner in tap_corners():
        window = take_window(padded, corner, extent)
        blocks.append(
            lax.dot_general(
                window, grad_rows, (((0,), (0,)), ((), ())), preferred_element_type=jnp.float32
            )
        )
    return jnp.concatenate(blocks, axis=0)


def adam_update(master, moment, second, teacher, gradient):
    new_moment = beta_first * moment + (1.0 - beta_first) * gradient
    new_second = beta_second * second + (1.0 - beta_second) * gradient * gradient
    first_fix = 1.0 - beta_first**STEP_COUNT
    second_fix = 1.0 - beta_second**STEP_COUNT
    ratio = new_moment / first_fix / (jnp.sqrt(new_second / second_fix) + adam_epsilon)
    new_master = master - learning_rate * (ratio + weight_decay * master)
    new_teacher = teacher_keep * teacher + (1.0 - teacher_keep) * new_master
    return (new_master, new_moment, new_second, new_teacher)


def local(voxels, occupancy, out_grad, weights, master, moment, second, teacher):
    own_cells = voxels[0]
    extent = tuple(own_cells.shape[:3])
    occupied = occupancy[0].astype(jnp.float32)[..., None]
    plane_pad = ((1, 1), (1, 1), (0, 0), (0, 0))
    rim_input = with_halo(own_cells, ((COLUMN_AXES, 2),), 1)
    padded_in = jnp.pad(rim_input, plane_pad)
    pre_one = forward_conv(padded_in, weights[0], extent)
    act_one = (occupied * jax.nn.silu(pre_one)).astype(jnp.bfloat16)
    rim_hidden = with_halo(act_one, ((COLUMN_AXES, 2),), 1)
    padded_act = jnp.pad(rim_hidden, plane_pad)
    pre_two = forward_conv(padded_act, weights[1], extent)
    grad_two = (out_grad[0].astype(jnp.float32) * occupied * silu_slope(pre_two)).astype(
        jnp.bfloat16
    )
    rim_grad = with_halo(grad_two, ((COLUMN_AXES, 2),), 1)
    padded_grad = jnp.pad(rim_grad, plane_pad)
    wgrad_two = weight_grad(padded_act, grad_two, extent)
    back_one = transposed_conv(padded_grad, weights[1], extent)
    grad_one = (back_one * occupied * silu_slope(pre_one)).astype(jnp.bfloat16)
    wgrad_one = weight_grad(padded_in, grad_one, extent)
    weight_grads = jnp.stack([wgrad_one, wgrad_two])
    gradient = scatter_rows_and_columns(weight_grads, master.shape)
    new_master, new_moment, new_second, new_teacher = adam_update(
        master, moment, second, teacher, gradient
    )
    fresh_weights = new_master.astype(jnp.bfloat16)
    new_weights = gather_rows(fresh_weights)
    return (new_master, new_moment, new_second, new_teacher, new_weights)


ROW_AXES = ("z", "x_lo", "core")
COLUMN_AXES = ("y", "x_hi")


def exchange_and_sum(blocks, axes):
    moved = lax.all_to_all(blocks, axes, 0, 0, tiled=True)
    return moved.sum(axis=0)


def scatter_rows_and_columns(weight_grads, own_shape):
    layers, rows, cols = own_shape
    lanes = weight_grads.shape[-1]
    z, x_lo, core = (lax.axis_size(name) for name in ROW_AXES)
    y, x_hi = (lax.axis_size(name) for name in COLUMN_AXES)
    blocks = weight_grads.reshape(layers, z, x_lo, core, rows, lanes)
    blocks = blocks.transpose(3, 2, 1, 0, 4, 5)
    blocks = exchange_and_sum(blocks, "core")
    blocks = exchange_and_sum(blocks, "x_lo")
    blocks = exchange_and_sum(blocks, "z")
    blocks = blocks.reshape(layers, rows, y * x_hi, cols).transpose(2, 0, 1, 3)
    blocks = exchange_and_sum(blocks, COLUMN_AXES)
    return blocks * unit_scale()


def gather_rows(fresh_weights):
    layers, rows, cols = fresh_weights.shape
    gathered = lax.all_gather(fresh_weights, "z", axis=0)
    gathered = lax.all_gather(gathered, ("x_lo", "core"), axis=0)
    gathered = gathered.reshape((-1,) + gathered.shape[1:])
    x_lo, core = lax.axis_size("x_lo"), lax.axis_size("core")
    gathered = gathered.reshape((x_lo, core) + gathered.shape[1:])
    gathered = gathered.transpose(3, 2, 0, 1, 4, 5)
    return gathered.reshape(layers, -1, cols)


def solution(mesh):
    rows_over, columns_over = mesh.shape["dp"], mesh.shape["slab"]
    fine = jax.sharding.Mesh(
        mesh.devices.reshape(rows_over // 4, 2, 2, columns_over // 2, 2), ROW_AXES + COLUMN_AXES
    )
    dp, slab = ROW_AXES, COLUMN_AXES
    in_specs = (
        P(dp, None, None, slab, None),
        P(dp, None, None, slab),
        P(dp, None, None, slab, None),
        P(),
        P(None, dp, slab),
        P(None, dp, slab),
        P(None, dp, slab),
        P(None, dp, slab),
    )
    out_specs = (
        P(None, dp, slab),
        P(None, dp, slab),
        P(None, dp, slab),
        P(None, dp, slab),
        P(None, None, slab),
    )
    return jax.shard_map(local, mesh=fine, in_specs=in_specs, out_specs=out_specs, check_vma=False)
```

```python
import jax
import jax.numpy as jnp
from jax import lax
from jax.sharding import PartitionSpec as P

C = 128
TAPS = 27
STEP_COUNT = 10


beta_first = 0.9
beta_second = 0.999
learning_rate = 0.01
weight_decay = 0.05
teacher_keep = 0.99
adam_epsilon = 1e-08


def with_halo(cells, sides, width):
    for axis, dim in sides:
        count = lax.axis_size(axis)
        ends = count - 1
        head = lax.slice_in_dim(cells, 0, width, axis=dim)
        tail = lax.slice_in_dim(cells, cells.shape[dim] - width, cells.shape[dim], axis=dim)
        cells = jnp.concatenate(
            [
                lax.ppermute(tail, axis, [(i, (i + 1) % count) for i in range(ends)]),
                cells,
                lax.ppermute(head, axis, [((i + 1) % count, i) for i in range(ends)]),
            ],
            axis=dim,
        )
    return cells


def tap_corners():
    return [
        (along_x, along_y, along_z)
        for along_x in range(3)
        for along_y in range(3)
        for along_z in range(3)
    ]


def unit_scale():
    return (TAPS * C) ** (-0.5)


def silu_slope(values):
    logistic = jax.nn.sigmoid(values)
    return logistic * (1.0 + values * (1.0 - logistic))


def take_window(padded, start, extent):
    window = padded[
        start[0] : start[0] + extent[0],
        start[1] : start[1] + extent[1],
        start[2] : start[2] + extent[2],
    ]
    return window.reshape(-1, window.shape[-1])


def forward_conv(padded, weight_rows, extent):
    channels = weight_rows.shape[1]
    summed = jnp.zeros((extent[0] * extent[1] * extent[2], channels), jnp.float32)
    for tap_index, corner in enumerate(tap_corners()):
        window = take_window(padded, corner, extent)
        block = weight_rows[tap_index * channels : (tap_index + 1) * channels]
        summed = summed + jnp.dot(window, block, preferred_element_type=jnp.float32)
    return (summed * unit_scale()).reshape(extent + (channels,))


def transposed_conv(padded_grad, weight_rows, extent):
    channels = weight_rows.shape[1]
    summed = jnp.zeros((extent[0] * extent[1] * extent[2], channels), jnp.float32)
    for tap_index, corner in enumerate(tap_corners()):
        start = (2 - corner[0], 2 - corner[1], 2 - corner[2])
        window = take_window(padded_grad, start, extent)
        block = weight_rows[tap_index * channels : (tap_index + 1) * channels]
        summed = summed + lax.dot_general(
            window, block, (((1,), (1,)), ((), ())), preferred_element_type=jnp.float32
        )
    return (summed * unit_scale()).reshape(extent + (channels,))


def weight_grad(padded, grad_field, extent):
    grad_rows = grad_field.reshape(-1, grad_field.shape[-1])
    blocks = []
    for corner in tap_corners():
        window = take_window(padded, corner, extent)
        blocks.append(
            lax.dot_general(
                window, grad_rows, (((0,), (0,)), ((), ())), preferred_element_type=jnp.float32
            )
        )
    return jnp.concatenate(blocks, axis=0)


def adam_update(master, moment, second, teacher, gradient):
    new_moment = beta_first * moment + (1.0 - beta_first) * gradient
    new_second = beta_second * second + (1.0 - beta_second) * gradient * gradient
    first_fix = 1.0 - beta_first**STEP_COUNT
    second_fix = 1.0 - beta_second**STEP_COUNT
    ratio = new_moment / first_fix / (jnp.sqrt(new_second / second_fix) + adam_epsilon)
    new_master = master - learning_rate * (ratio + weight_decay * master)
    new_teacher = teacher_keep * teacher + (1.0 - teacher_keep) * new_master
    return (new_master, new_moment, new_second, new_teacher)


def local(voxels, occupancy, out_grad, weights, master, moment, second, teacher):
    own_cells = voxels[0]
    extent = tuple(own_cells.shape[:3])
    occupied = occupancy[0].astype(jnp.float32)[..., None]
    plane_pad = ((1, 1), (1, 1), (0, 0), (0, 0))
    rim_input = with_halo(own_cells, ((COLUMN_AXES, 2),), 1)
    padded_in = jnp.pad(rim_input, plane_pad)
    pre_one = forward_conv(padded_in, weights[0], extent)
    act_one = (occupied * jax.nn.silu(pre_one)).astype(jnp.bfloat16)
    rim_hidden = with_halo(act_one, ((COLUMN_AXES, 2),), 1)
    padded_act = jnp.pad(rim_hidden, plane_pad)
    pre_two = forward_conv(padded_act, weights[1], extent)
    grad_two = (out_grad[0].astype(jnp.float32) * occupied * silu_slope(pre_two)).astype(
        jnp.bfloat16
    )
    rim_grad = with_halo(grad_two, ((COLUMN_AXES, 2),), 1)
    padded_grad = jnp.pad(rim_grad, plane_pad)
    wgrad_two = weight_grad(padded_act, grad_two, extent)
    back_one = transposed_conv(padded_grad, weights[1], extent)
    grad_one = (back_one * occupied * silu_slope(pre_one)).astype(jnp.bfloat16)
    wgrad_one = weight_grad(padded_in, grad_one, extent)
    weight_grads = jnp.stack([wgrad_one, wgrad_two])
    gradient = scatter_rows_and_columns(weight_grads, master.shape)
    new_master, new_moment, new_second, new_teacher = adam_update(
        master, moment, second, teacher, gradient
    )
    fresh_weights = new_master.astype(jnp.bfloat16)
    new_weights = gather_rows(fresh_weights)
    return (new_master, new_moment, new_second, new_teacher, new_weights)


ROW_AXES = ("z_hi", "z_lo", "x_lo", "core")
COLUMN_AXES = ("y", "x_hi")


def exchange_and_sum(blocks, axes):
    moved = lax.all_to_all(blocks, axes, 0, 0, tiled=True)
    return moved.sum(axis=0)


def scatter_rows_and_columns(weight_grads, own_shape):
    layers, rows, cols = own_shape
    lanes = weight_grads.shape[-1]
    z_hi, z_lo, x_lo, core = (lax.axis_size(name) for name in ROW_AXES)
    y, x_hi = (lax.axis_size(name) for name in COLUMN_AXES)
    blocks = weight_grads.reshape(layers, z_hi, z_lo, x_lo, core, rows, lanes)
    blocks = blocks.transpose(4, 3, 2, 1, 0, 5, 6)
    blocks = exchange_and_sum(blocks, "core")
    blocks = exchange_and_sum(blocks, "x_lo")
    blocks = exchange_and_sum(blocks, "z_lo")
    blocks = exchange_and_sum(blocks, "z_hi")
    blocks = blocks.reshape(layers, rows, y * x_hi, cols).transpose(2, 0, 1, 3)
    blocks = exchange_and_sum(blocks, COLUMN_AXES)
    return blocks * unit_scale()


def gather_rows(fresh_weights):
    layers, rows, cols = fresh_weights.shape
    gathered = fresh_weights
    for name in ROW_AXES:
        gathered = lax.all_gather(gathered, name, axis=0)
    gathered = gathered.transpose(4, 3, 2, 1, 0, 5, 6)
    return gathered.reshape(layers, -1, cols)


def solution(mesh):
    rows_over, columns_over = mesh.shape["dp"], mesh.shape["slab"]
    fine = jax.sharding.Mesh(
        mesh.devices.reshape(rows_over // 16, 4, 2, 2, columns_over // 2, 2), ROW_AXES + COLUMN_AXES
    )
    dp, slab = ROW_AXES, COLUMN_AXES
    in_specs = (
        P(dp, None, None, slab, None),
        P(dp, None, None, slab),
        P(dp, None, None, slab, None),
        P(),
        P(None, dp, slab),
        P(None, dp, slab),
        P(None, dp, slab),
        P(None, dp, slab),
    )
    out_specs = (
        P(None, dp, slab),
        P(None, dp, slab),
        P(None, dp, slab),
        P(None, dp, slab),
        P(None, None, slab),
    )
    return jax.shard_map(local, mesh=fine, in_specs=in_specs, out_specs=out_specs, check_vma=False)
```

```python
import jax
import jax.numpy as jnp
from jax import lax
from jax.sharding import PartitionSpec as P

C = 128
TAPS = 27
STEP_COUNT = 10


beta_first = 0.9
beta_second = 0.999
learning_rate = 0.01
weight_decay = 0.05
teacher_keep = 0.99
adam_epsilon = 1e-08


def with_halo(cells, sides, width):
    for axis, dim in sides:
        count = lax.axis_size(axis)
        ends = count - 1
        head = lax.slice_in_dim(cells, 0, width, axis=dim)
        tail = lax.slice_in_dim(cells, cells.shape[dim] - width, cells.shape[dim], axis=dim)
        cells = jnp.concatenate(
            [
                lax.ppermute(tail, axis, [(i, (i + 1) % count) for i in range(ends)]),
                cells,
                lax.ppermute(head, axis, [((i + 1) % count, i) for i in range(ends)]),
            ],
            axis=dim,
        )
    return cells


def tap_corners():
    return [
        (along_x, along_y, along_z)
        for along_x in range(3)
        for along_y in range(3)
        for along_z in range(3)
    ]


def unit_scale():
    return (TAPS * C) ** (-0.5)


def silu_slope(values):
    logistic = jax.nn.sigmoid(values)
    return logistic * (1.0 + values * (1.0 - logistic))


def take_window(padded, start, extent):
    window = padded[
        start[0] : start[0] + extent[0],
        start[1] : start[1] + extent[1],
        start[2] : start[2] + extent[2],
    ]
    return window.reshape(-1, window.shape[-1])


def forward_conv(padded, weight_rows, extent):
    channels = weight_rows.shape[1]
    summed = jnp.zeros((extent[0] * extent[1] * extent[2], channels), jnp.float32)
    for tap_index, corner in enumerate(tap_corners()):
        window = take_window(padded, corner, extent)
        block = weight_rows[tap_index * channels : (tap_index + 1) * channels]
        summed = summed + jnp.dot(window, block, preferred_element_type=jnp.float32)
    return (summed * unit_scale()).reshape(extent + (channels,))


def transposed_conv(padded_grad, weight_rows, extent):
    channels = weight_rows.shape[1]
    summed = jnp.zeros((extent[0] * extent[1] * extent[2], channels), jnp.float32)
    for tap_index, corner in enumerate(tap_corners()):
        start = (2 - corner[0], 2 - corner[1], 2 - corner[2])
        window = take_window(padded_grad, start, extent)
        block = weight_rows[tap_index * channels : (tap_index + 1) * channels]
        summed = summed + lax.dot_general(
            window, block, (((1,), (1,)), ((), ())), preferred_element_type=jnp.float32
        )
    return (summed * unit_scale()).reshape(extent + (channels,))


def weight_grad(padded, grad_field, extent):
    grad_rows = grad_field.reshape(-1, grad_field.shape[-1])
    blocks = []
    for corner in tap_corners():
        window = take_window(padded, corner, extent)
        blocks.append(
            lax.dot_general(
                window, grad_rows, (((0,), (0,)), ((), ())), preferred_element_type=jnp.float32
            )
        )
    return jnp.concatenate(blocks, axis=0)


def adam_update(master, moment, second, teacher, gradient):
    new_moment = beta_first * moment + (1.0 - beta_first) * gradient
    new_second = beta_second * second + (1.0 - beta_second) * gradient * gradient
    first_fix = 1.0 - beta_first**STEP_COUNT
    second_fix = 1.0 - beta_second**STEP_COUNT
    ratio = new_moment / first_fix / (jnp.sqrt(new_second / second_fix) + adam_epsilon)
    new_master = master - learning_rate * (ratio + weight_decay * master)
    new_teacher = teacher_keep * teacher + (1.0 - teacher_keep) * new_master
    return (new_master, new_moment, new_second, new_teacher)


def local(voxels, occupancy, out_grad, weights, master, moment, second, teacher):
    own_cells = voxels[0]
    extent = tuple(own_cells.shape[:3])
    occupied = occupancy[0].astype(jnp.float32)[..., None]
    plane_pad = ((1, 1), (1, 1), (0, 0), (0, 0))
    rim_input = with_halo(own_cells, ((COLUMN_AXES, 2),), 1)
    padded_in = jnp.pad(rim_input, plane_pad)
    pre_one = forward_conv(padded_in, weights[0], extent)
    act_one = (occupied * jax.nn.silu(pre_one)).astype(jnp.bfloat16)
    rim_hidden = with_halo(act_one, ((COLUMN_AXES, 2),), 1)
    padded_act = jnp.pad(rim_hidden, plane_pad)
    pre_two = forward_conv(padded_act, weights[1], extent)
    grad_two = (out_grad[0].astype(jnp.float32) * occupied * silu_slope(pre_two)).astype(
        jnp.bfloat16
    )
    rim_grad = with_halo(grad_two, ((COLUMN_AXES, 2),), 1)
    padded_grad = jnp.pad(rim_grad, plane_pad)
    cols = master.shape[-1]
    scene_in = whole_scene(own_cells)
    scene_act = whole_scene(act_one)
    scene_extent = tuple(scene_in.shape[:3])
    wgrad_two = weight_grad(pad_scene(scene_act), own_columns(grad_two, cols), scene_extent)
    back_one = transposed_conv(padded_grad, weights[1], extent)
    grad_one = (back_one * occupied * silu_slope(pre_one)).astype(jnp.bfloat16)
    wgrad_one = weight_grad(pad_scene(scene_in), own_columns(grad_one, cols), scene_extent)
    weight_grads = jnp.stack([wgrad_one, wgrad_two])
    gradient = scatter_rows_and_columns(weight_grads, master.shape)
    new_master, new_moment, new_second, new_teacher = adam_update(
        master, moment, second, teacher, gradient
    )
    fresh_weights = new_master.astype(jnp.bfloat16)
    new_weights = gather_rows(fresh_weights)
    return (new_master, new_moment, new_second, new_teacher, new_weights)


ROW_AXES = ("z", "x_lo", "core")
COLUMN_AXES = ("y", "x_hi")


def exchange_and_sum(blocks, axes):
    moved = lax.all_to_all(blocks, axes, 0, 0, tiled=True)
    return moved.sum(axis=0)


def whole_scene(cells):
    return lax.all_gather(cells, COLUMN_AXES, axis=2, tiled=True)


def pad_scene(cells):
    return jnp.pad(cells, ((1, 1), (1, 1), (1, 1), (0, 0)))


def own_columns(field, cols):
    split = field.reshape(field.shape[:3] + (field.shape[3] // cols, cols))
    moved = lax.all_to_all(split, COLUMN_AXES, 3, 2, tiled=True)
    return moved.reshape(moved.shape[:3] + (cols,))


def scatter_rows_and_columns(weight_grads, own_shape):
    layers, rows, cols = own_shape
    z, x_lo, core = (lax.axis_size(name) for name in ROW_AXES)
    blocks = weight_grads.reshape(layers, z, x_lo, core, rows, cols)
    blocks = blocks.transpose(3, 2, 1, 0, 4, 5).reshape(core, x_lo, z, layers, rows * cols)
    blocks = exchange_and_sum(blocks, "core")
    blocks = exchange_and_sum(blocks, "x_lo")
    blocks = exchange_and_sum(blocks, "z")
    return blocks.reshape(own_shape) * unit_scale()


def gather_rows(fresh_weights):
    layers, rows, cols = fresh_weights.shape
    gathered = lax.all_gather(fresh_weights, "z", axis=0)
    gathered = lax.all_gather(gathered, ("x_lo", "core"), axis=0)
    gathered = gathered.reshape((-1,) + gathered.shape[1:])
    x_lo, core = lax.axis_size("x_lo"), lax.axis_size("core")
    gathered = gathered.reshape((x_lo, core) + gathered.shape[1:])
    gathered = gathered.transpose(3, 2, 0, 1, 4, 5)
    return gathered.reshape(layers, -1, cols)


def solution(mesh):
    rows_over, columns_over = mesh.shape["dp"], mesh.shape["slab"]
    fine = jax.sharding.Mesh(
        mesh.devices.reshape(rows_over // 4, 2, 2, columns_over // 2, 2), ROW_AXES + COLUMN_AXES
    )
    dp, slab = ROW_AXES, COLUMN_AXES
    in_specs = (
        P(dp, None, None, slab, None),
        P(dp, None, None, slab),
        P(dp, None, None, slab, None),
        P(),
        P(None, dp, slab),
        P(None, dp, slab),
        P(None, dp, slab),
        P(None, dp, slab),
    )
    out_specs = (
        P(None, dp, slab),
        P(None, dp, slab),
        P(None, dp, slab),
        P(None, dp, slab),
        P(None, None, slab),
    )
    return jax.shard_map(local, mesh=fine, in_specs=in_specs, out_specs=out_specs, check_vma=False)
```

```python
import jax
import jax.numpy as jnp
from jax import lax
from jax.sharding import PartitionSpec as P

C = 128
TAPS = 27
STEP_COUNT = 10


beta_first = 0.9
beta_second = 0.999
learning_rate = 0.01
weight_decay = 0.05
teacher_keep = 0.99
adam_epsilon = 1e-08


def with_halo(cells, sides, width):
    for axis, dim in sides:
        count = lax.axis_size(axis)
        ends = count - 1
        head = lax.slice_in_dim(cells, 0, width, axis=dim)
        tail = lax.slice_in_dim(cells, cells.shape[dim] - width, cells.shape[dim], axis=dim)
        cells = jnp.concatenate(
            [
                lax.ppermute(tail, axis, [(i, (i + 1) % count) for i in range(ends)]),
                cells,
                lax.ppermute(head, axis, [((i + 1) % count, i) for i in range(ends)]),
            ],
            axis=dim,
        )
    return cells


def tap_corners():
    return [
        (along_x, along_y, along_z)
        for along_x in range(3)
        for along_y in range(3)
        for along_z in range(3)
    ]


def unit_scale():
    return (TAPS * C) ** (-0.5)


def silu_slope(values):
    logistic = jax.nn.sigmoid(values)
    return logistic * (1.0 + values * (1.0 - logistic))


def take_window(padded, start, extent):
    window = padded[
        start[0] : start[0] + extent[0],
        start[1] : start[1] + extent[1],
        start[2] : start[2] + extent[2],
    ]
    return window.reshape(-1, window.shape[-1])


def forward_conv(padded, weight_rows, extent):
    channels = weight_rows.shape[1]
    summed = jnp.zeros((extent[0] * extent[1] * extent[2], channels), jnp.float32)
    for tap_index, corner in enumerate(tap_corners()):
        window = take_window(padded, corner, extent)
        block = weight_rows[tap_index * channels : (tap_index + 1) * channels]
        summed = summed + jnp.dot(window, block, preferred_element_type=jnp.float32)
    return (summed * unit_scale()).reshape(extent + (channels,))


def transposed_conv(padded_grad, weight_rows, extent):
    channels = weight_rows.shape[1]
    summed = jnp.zeros((extent[0] * extent[1] * extent[2], channels), jnp.float32)
    for tap_index, corner in enumerate(tap_corners()):
        start = (2 - corner[0], 2 - corner[1], 2 - corner[2])
        window = take_window(padded_grad, start, extent)
        block = weight_rows[tap_index * channels : (tap_index + 1) * channels]
        summed = summed + lax.dot_general(
            window, block, (((1,), (1,)), ((), ())), preferred_element_type=jnp.float32
        )
    return (summed * unit_scale()).reshape(extent + (channels,))


def weight_grad(padded, grad_field, extent):
    grad_rows = grad_field.reshape(-1, grad_field.shape[-1])
    blocks = []
    for corner in tap_corners():
        window = take_window(padded, corner, extent)
        blocks.append(
            lax.dot_general(
                window, grad_rows, (((0,), (0,)), ((), ())), preferred_element_type=jnp.float32
            )
        )
    return jnp.concatenate(blocks, axis=0)


def adam_update(master, moment, second, teacher, gradient):
    new_moment = beta_first * moment + (1.0 - beta_first) * gradient
    new_second = beta_second * second + (1.0 - beta_second) * gradient * gradient
    first_fix = 1.0 - beta_first**STEP_COUNT
    second_fix = 1.0 - beta_second**STEP_COUNT
    ratio = new_moment / first_fix / (jnp.sqrt(new_second / second_fix) + adam_epsilon)
    new_master = master - learning_rate * (ratio + weight_decay * master)
    new_teacher = teacher_keep * teacher + (1.0 - teacher_keep) * new_master
    return (new_master, new_moment, new_second, new_teacher)


def local(voxels, occupancy, out_grad, weights, master, moment, second, teacher):
    own_cells = voxels[0]
    extent = tuple(own_cells.shape[:3])
    occupied = occupancy[0].astype(jnp.float32)[..., None]
    plane_pad = ((1, 1), (1, 1), (0, 0), (0, 0))
    rim_input = with_halo(own_cells, ((COLUMN_AXES, 2),), 1)
    padded_in = jnp.pad(rim_input, plane_pad)
    pre_one = forward_conv(padded_in, weights[0], extent)
    act_one = (occupied * jax.nn.silu(pre_one)).astype(jnp.bfloat16)
    rim_hidden = with_halo(act_one, ((COLUMN_AXES, 2),), 1)
    padded_act = jnp.pad(rim_hidden, plane_pad)
    pre_two = forward_conv(padded_act, weights[1], extent)
    grad_two = (out_grad[0].astype(jnp.float32) * occupied * silu_slope(pre_two)).astype(
        jnp.bfloat16
    )
    rim_grad = with_halo(grad_two, ((COLUMN_AXES, 2),), 1)
    padded_grad = jnp.pad(rim_grad, plane_pad)
    cols = master.shape[-1]
    scene_in = whole_scene(own_cells)
    scene_act = whole_scene(act_one)
    scene_extent = tuple(scene_in.shape[:3])
    wgrad_two = weight_grad(pad_scene(scene_act), own_columns(grad_two, cols), scene_extent)
    back_one = transposed_conv(padded_grad, weights[1], extent)
    grad_one = (back_one * occupied * silu_slope(pre_one)).astype(jnp.bfloat16)
    wgrad_one = weight_grad(pad_scene(scene_in), own_columns(grad_one, cols), scene_extent)
    weight_grads = jnp.stack([wgrad_one, wgrad_two])
    gradient = scatter_rows_and_columns(weight_grads, master.shape)
    new_master, new_moment, new_second, new_teacher = adam_update(
        master, moment, second, teacher, gradient
    )
    fresh_weights = new_master.astype(jnp.bfloat16)
    new_weights = gather_rows(fresh_weights)
    return (new_master, new_moment, new_second, new_teacher, new_weights)


ROW_AXES = ("z", "x_lo", "core")
COLUMN_AXES = ("y", "x_hi")


def exchange_and_sum(blocks, axes):
    moved = lax.all_to_all(blocks, axes, 0, 0, tiled=True)
    return moved.sum(axis=0)


def whole_scene(cells):
    parts = 1
    for name in COLUMN_AXES:
        parts *= lax.axis_size(name)
    copies = jnp.broadcast_to(cells[None], (parts,) + cells.shape)
    return lax.all_to_all(copies, COLUMN_AXES, 0, 3, tiled=True)[0]


def pad_scene(cells):
    return jnp.pad(cells, ((1, 1), (1, 1), (1, 1), (0, 0)))


def own_columns(field, cols):
    split = field.reshape(field.shape[:3] + (field.shape[3] // cols, cols))
    moved = lax.all_to_all(split, COLUMN_AXES, 3, 2, tiled=True)
    return moved.reshape(moved.shape[:3] + (cols,))


def scatter_rows_and_columns(weight_grads, own_shape):
    layers, rows, cols = own_shape
    z, x_lo, core = (lax.axis_size(name) for name in ROW_AXES)
    blocks = weight_grads.reshape(layers, z, x_lo, core, rows, cols)
    blocks = blocks.transpose(3, 2, 1, 0, 4, 5).reshape(core, x_lo, z, layers, rows * cols)
    blocks = exchange_and_sum(blocks, "core")
    blocks = exchange_and_sum(blocks, "x_lo")
    blocks = exchange_and_sum(blocks, "z")
    return blocks.reshape(own_shape) * unit_scale()


def gather_rows(fresh_weights):
    layers, rows, cols = fresh_weights.shape
    gathered = lax.all_gather(fresh_weights, "z", axis=0)
    gathered = lax.all_gather(gathered, ("x_lo", "core"), axis=0)
    gathered = gathered.reshape((-1,) + gathered.shape[1:])
    x_lo, core = lax.axis_size("x_lo"), lax.axis_size("core")
    gathered = gathered.reshape((x_lo, core) + gathered.shape[1:])
    gathered = gathered.transpose(3, 2, 0, 1, 4, 5)
    return gathered.reshape(layers, -1, cols)


def solution(mesh):
    rows_over, columns_over = mesh.shape["dp"], mesh.shape["slab"]
    fine = jax.sharding.Mesh(
        mesh.devices.reshape(rows_over // 4, 2, 2, columns_over // 2, 2), ROW_AXES + COLUMN_AXES
    )
    dp, slab = ROW_AXES, COLUMN_AXES
    in_specs = (
        P(dp, None, None, slab, None),
        P(dp, None, None, slab),
        P(dp, None, None, slab, None),
        P(),
        P(None, dp, slab),
        P(None, dp, slab),
        P(None, dp, slab),
        P(None, dp, slab),
    )
    out_specs = (
        P(None, dp, slab),
        P(None, dp, slab),
        P(None, dp, slab),
        P(None, dp, slab),
        P(None, None, slab),
    )
    return jax.shard_map(local, mesh=fine, in_specs=in_specs, out_specs=out_specs, check_vma=False)
```

```python
import jax
import jax.numpy as jnp
from jax import lax
from jax.sharding import PartitionSpec as P

C = 128
TAPS = 27
STEP_COUNT = 10


beta_first = 0.9
beta_second = 0.999
learning_rate = 0.01
weight_decay = 0.05
teacher_keep = 0.99
adam_epsilon = 1e-08


def with_halo(cells, sides, width):
    for axis, dim in sides:
        count = lax.axis_size(axis)
        ends = count - 1
        head = lax.slice_in_dim(cells, 0, width, axis=dim)
        tail = lax.slice_in_dim(cells, cells.shape[dim] - width, cells.shape[dim], axis=dim)
        cells = jnp.concatenate(
            [
                lax.ppermute(tail, axis, [(i, (i + 1) % count) for i in range(ends)]),
                cells,
                lax.ppermute(head, axis, [((i + 1) % count, i) for i in range(ends)]),
            ],
            axis=dim,
        )
    return cells


def tap_corners():
    return [
        (along_x, along_y, along_z)
        for along_x in range(3)
        for along_y in range(3)
        for along_z in range(3)
    ]


def unit_scale():
    return (TAPS * C) ** (-0.5)


def silu_slope(values):
    logistic = jax.nn.sigmoid(values)
    return logistic * (1.0 + values * (1.0 - logistic))


def take_window(padded, start, extent):
    window = padded[
        start[0] : start[0] + extent[0],
        start[1] : start[1] + extent[1],
        start[2] : start[2] + extent[2],
    ]
    return window.reshape(-1, window.shape[-1])


def stacked_windows(padded, starts, extent):
    return jnp.concatenate([take_window(padded, start, extent) for start in starts], axis=-1)


def forward_conv(padded, weight_rows, extent):
    channels = weight_rows.shape[1]
    columns = stacked_windows(padded, tap_corners(), extent)
    summed = jnp.dot(columns, weight_rows, preferred_element_type=jnp.float32)
    return (summed * unit_scale()).reshape(extent + (channels,))


def transposed_conv(padded_grad, weight_rows, extent):
    channels = weight_rows.shape[1]
    starts = [(2 - a, 2 - b, 2 - c) for a, b, c in tap_corners()]
    columns = stacked_windows(padded_grad, starts, extent)
    flipped = weight_rows.reshape(TAPS, channels, channels).transpose(0, 2, 1)
    summed = jnp.dot(
        columns, flipped.reshape(TAPS * channels, channels), preferred_element_type=jnp.float32
    )
    return (summed * unit_scale()).reshape(extent + (channels,))


def weight_grad(padded, grad_field, extent):
    grad_rows = grad_field.reshape(-1, grad_field.shape[-1])
    columns = stacked_windows(padded, tap_corners(), extent)
    return lax.dot_general(
        columns, grad_rows, (((0,), (0,)), ((), ())), preferred_element_type=jnp.float32
    )


def adam_update(master, moment, second, teacher, gradient):
    new_moment = beta_first * moment + (1.0 - beta_first) * gradient
    new_second = beta_second * second + (1.0 - beta_second) * gradient * gradient
    first_fix = 1.0 - beta_first**STEP_COUNT
    second_fix = 1.0 - beta_second**STEP_COUNT
    ratio = new_moment / first_fix / (jnp.sqrt(new_second / second_fix) + adam_epsilon)
    new_master = master - learning_rate * (ratio + weight_decay * master)
    new_teacher = teacher_keep * teacher + (1.0 - teacher_keep) * new_master
    return (new_master, new_moment, new_second, new_teacher)


def local(voxels, occupancy, out_grad, weights, master, moment, second, teacher):
    own_cells = voxels[0]
    extent = tuple(own_cells.shape[:3])
    occupied = occupancy[0].astype(jnp.float32)[..., None]
    plane_pad = ((1, 1), (1, 1), (0, 0), (0, 0))
    rim_input = with_halo(own_cells, ((COLUMN_AXES, 2),), 1)
    padded_in = jnp.pad(rim_input, plane_pad)
    pre_one = forward_conv(padded_in, weights[0], extent)
    act_one = (occupied * jax.nn.silu(pre_one)).astype(jnp.bfloat16)
    rim_hidden = with_halo(act_one, ((COLUMN_AXES, 2),), 1)
    padded_act = jnp.pad(rim_hidden, plane_pad)
    pre_two = forward_conv(padded_act, weights[1], extent)
    grad_two = (out_grad[0].astype(jnp.float32) * occupied * silu_slope(pre_two)).astype(
        jnp.bfloat16
    )
    rim_grad = with_halo(grad_two, ((COLUMN_AXES, 2),), 1)
    padded_grad = jnp.pad(rim_grad, plane_pad)
    wgrad_two = weight_grad(padded_act, grad_two, extent)
    back_one = transposed_conv(padded_grad, weights[1], extent)
    grad_one = (back_one * occupied * silu_slope(pre_one)).astype(jnp.bfloat16)
    wgrad_one = weight_grad(padded_in, grad_one, extent)
    weight_grads = jnp.stack([wgrad_one, wgrad_two])
    gradient = scatter_rows_and_columns(weight_grads, master.shape)
    new_master, new_moment, new_second, new_teacher = adam_update(
        master, moment, second, teacher, gradient
    )
    fresh_weights = new_master.astype(jnp.bfloat16)
    new_weights = gather_rows(fresh_weights)
    return (new_master, new_moment, new_second, new_teacher, new_weights)


ROW_AXES = ("z", "x_lo", "core")
COLUMN_AXES = ("y", "x_hi")


def exchange_and_sum(blocks, axes):
    moved = lax.all_to_all(blocks, axes, 0, 0, tiled=True)
    return moved.sum(axis=0)


def scatter_rows_and_columns(weight_grads, own_shape):
    layers, rows, cols = own_shape
    lanes = weight_grads.shape[-1]
    z, x_lo, core = (lax.axis_size(name) for name in ROW_AXES)
    y, x_hi = (lax.axis_size(name) for name in COLUMN_AXES)
    blocks = weight_grads.reshape(layers, z, x_lo, core, rows, lanes)
    blocks = blocks.transpose(3, 2, 1, 0, 4, 5)
    blocks = exchange_and_sum(blocks, "core")
    blocks = exchange_and_sum(blocks, "x_lo")
    blocks = exchange_and_sum(blocks, "z")
    blocks = blocks.reshape(layers, rows, y * x_hi, cols).transpose(2, 0, 1, 3)
    blocks = exchange_and_sum(blocks, COLUMN_AXES)
    return blocks * unit_scale()


def gather_rows(fresh_weights):
    layers, rows, cols = fresh_weights.shape
    gathered = lax.all_gather(fresh_weights, "z", axis=0)
    gathered = lax.all_gather(gathered, ("x_lo", "core"), axis=0)
    gathered = gathered.reshape((-1,) + gathered.shape[1:])
    x_lo, core = lax.axis_size("x_lo"), lax.axis_size("core")
    gathered = gathered.reshape((x_lo, core) + gathered.shape[1:])
    gathered = gathered.transpose(3, 2, 0, 1, 4, 5)
    return gathered.reshape(layers, -1, cols)


def solution(mesh):
    rows_over, columns_over = mesh.shape["dp"], mesh.shape["slab"]
    fine = jax.sharding.Mesh(
        mesh.devices.reshape(rows_over // 4, 2, 2, columns_over // 2, 2), ROW_AXES + COLUMN_AXES
    )
    dp, slab = ROW_AXES, COLUMN_AXES
    in_specs = (
        P(dp, None, None, slab, None),
        P(dp, None, None, slab),
        P(dp, None, None, slab, None),
        P(),
        P(None, dp, slab),
        P(None, dp, slab),
        P(None, dp, slab),
        P(None, dp, slab),
    )
    out_specs = (
        P(None, dp, slab),
        P(None, dp, slab),
        P(None, dp, slab),
        P(None, dp, slab),
        P(None, None, slab),
    )
    return jax.shard_map(local, mesh=fine, in_specs=in_specs, out_specs=out_specs, check_vma=False)
```

```python
import jax
import jax.numpy as jnp
from jax import lax
from jax.sharding import PartitionSpec as P

C = 128
TAPS = 27
STEP_COUNT = 10


beta_first = 0.9
beta_second = 0.999
learning_rate = 0.01
weight_decay = 0.05
teacher_keep = 0.99
adam_epsilon = 1e-08


def with_halo(cells, sides, width):
    for axis, dim in sides:
        count = lax.axis_size(axis)
        ends = count - 1
        head = lax.slice_in_dim(cells, 0, width, axis=dim)
        tail = lax.slice_in_dim(cells, cells.shape[dim] - width, cells.shape[dim], axis=dim)
        cells = jnp.concatenate(
            [
                lax.ppermute(tail, axis, [(i, (i + 1) % count) for i in range(ends)]),
                cells,
                lax.ppermute(head, axis, [((i + 1) % count, i) for i in range(ends)]),
            ],
            axis=dim,
        )
    return cells


def tap_corners():
    return [
        (along_x, along_y, along_z)
        for along_x in range(3)
        for along_y in range(3)
        for along_z in range(3)
    ]


def unit_scale():
    return (TAPS * C) ** (-0.5)


def silu_slope(values):
    logistic = jax.nn.sigmoid(values)
    return logistic * (1.0 + values * (1.0 - logistic))


def take_window(padded, start, extent):
    window = padded[
        start[0] : start[0] + extent[0],
        start[1] : start[1] + extent[1],
        start[2] : start[2] + extent[2],
    ]
    return window.reshape(-1, window.shape[-1])


def stacked_windows(padded, starts, extent):
    return jnp.concatenate([take_window(padded, start, extent) for start in starts], axis=-1)


def forward_conv(padded, weight_rows, extent):
    channels = weight_rows.shape[1]
    columns = stacked_windows(padded, tap_corners(), extent)
    summed = jnp.dot(columns, weight_rows, preferred_element_type=jnp.float32)
    return (summed * unit_scale()).reshape(extent + (channels,))


def transposed_conv(padded_grad, weight_rows, extent):
    channels = weight_rows.shape[1]
    starts = [(2 - a, 2 - b, 2 - c) for a, b, c in tap_corners()]
    columns = stacked_windows(padded_grad, starts, extent)
    flipped = weight_rows.reshape(TAPS, channels, channels).transpose(0, 2, 1)
    summed = jnp.dot(
        columns, flipped.reshape(TAPS * channels, channels), preferred_element_type=jnp.float32
    )
    return (summed * unit_scale()).reshape(extent + (channels,))


def weight_grad(padded, grad_field, extent):
    grad_rows = grad_field.reshape(-1, grad_field.shape[-1])
    columns = stacked_windows(padded, tap_corners(), extent)
    return lax.dot_general(
        columns, grad_rows, (((0,), (0,)), ((), ())), preferred_element_type=jnp.float32
    )


def adam_update(master, moment, second, teacher, gradient):
    new_moment = beta_first * moment + (1.0 - beta_first) * gradient
    new_second = beta_second * second + (1.0 - beta_second) * gradient * gradient
    first_fix = 1.0 - beta_first**STEP_COUNT
    second_fix = 1.0 - beta_second**STEP_COUNT
    ratio = new_moment / first_fix / (jnp.sqrt(new_second / second_fix) + adam_epsilon)
    new_master = master - learning_rate * (ratio + weight_decay * master)
    new_teacher = teacher_keep * teacher + (1.0 - teacher_keep) * new_master
    return (new_master, new_moment, new_second, new_teacher)


def local(voxels, occupancy, out_grad, weights, master, moment, second, teacher):
    own_cells = voxels[0]
    extent = tuple(own_cells.shape[:3])
    occupied = occupancy[0].astype(jnp.float32)[..., None]
    plane_pad = ((1, 1), (1, 1), (0, 0), (0, 0))
    rim_input = with_halo(own_cells, ((COLUMN_AXES, 2),), 1)
    padded_in = jnp.pad(rim_input, plane_pad)
    pre_one = forward_conv(padded_in, weights[0], extent)
    act_one = (occupied * jax.nn.silu(pre_one)).astype(jnp.bfloat16)
    rim_hidden = with_halo(act_one, ((COLUMN_AXES, 2),), 1)
    padded_act = jnp.pad(rim_hidden, plane_pad)
    pre_two = forward_conv(padded_act, weights[1], extent)
    grad_two = (out_grad[0].astype(jnp.float32) * occupied * silu_slope(pre_two)).astype(
        jnp.bfloat16
    )
    rim_grad = with_halo(grad_two, ((COLUMN_AXES, 2),), 1)
    padded_grad = jnp.pad(rim_grad, plane_pad)
    wgrad_two = weight_grad(padded_act, grad_two, extent)
    back_one = transposed_conv(padded_grad, weights[1], extent)
    grad_one = (back_one * occupied * silu_slope(pre_one)).astype(jnp.bfloat16)
    wgrad_one = weight_grad(padded_in, grad_one, extent)
    weight_grads = jnp.stack([wgrad_one, wgrad_two])
    gradient = scatter_rows_and_columns(weight_grads, master.shape)
    new_master, new_moment, new_second, new_teacher = adam_update(
        master, moment, second, teacher, gradient
    )
    fresh_weights = new_master.astype(jnp.bfloat16)
    new_weights = gather_rows(fresh_weights)
    return (new_master, new_moment, new_second, new_teacher, new_weights)


ROW_AXES = ("z", "x_lo", "core")
COLUMN_AXES = ("y", "x_hi")


def exchange_and_sum(blocks, axes):
    moved = lax.all_to_all(blocks, axes, 0, 0, tiled=True)
    return moved.sum(axis=0)


def scatter_rows_and_columns(weight_grads, own_shape):
    layers, rows, cols = own_shape
    lanes = weight_grads.shape[-1]
    z, x_lo, core = (lax.axis_size(name) for name in ROW_AXES)
    y, x_hi = (lax.axis_size(name) for name in COLUMN_AXES)
    blocks = weight_grads.reshape(layers, z, x_lo, core, rows, lanes)
    blocks = blocks.transpose(3, 2, 1, 0, 4, 5)
    blocks = exchange_and_sum(blocks, "core")
    blocks = exchange_and_sum(blocks, "x_lo")
    half = y * cols
    blocks = blocks.reshape(z, layers, rows, y, x_hi, cols).transpose(4, 0, 1, 2, 3, 5)
    blocks = blocks.reshape(x_hi, z, layers, rows * half // lanes, lanes)
    blocks = exchange_and_sum(blocks, "x_hi")
    blocks = exchange_and_sum(blocks, "z")
    blocks = blocks.reshape(layers, rows, y, cols).transpose(2, 0, 1, 3)
    blocks = exchange_and_sum(blocks, "y")
    return blocks * unit_scale()


def gather_rows(fresh_weights):
    layers, rows, cols = fresh_weights.shape
    gathered = lax.all_gather(fresh_weights, "z", axis=0)
    gathered = lax.all_gather(gathered, ("x_lo", "core"), axis=0)
    gathered = gathered.reshape((-1,) + gathered.shape[1:])
    x_lo, core = lax.axis_size("x_lo"), lax.axis_size("core")
    gathered = gathered.reshape((x_lo, core) + gathered.shape[1:])
    gathered = gathered.transpose(3, 2, 0, 1, 4, 5)
    return gathered.reshape(layers, -1, cols)


def solution(mesh):
    rows_over, columns_over = mesh.shape["dp"], mesh.shape["slab"]
    fine = jax.sharding.Mesh(
        mesh.devices.reshape(rows_over // 4, 2, 2, columns_over // 2, 2), ROW_AXES + COLUMN_AXES
    )
    dp, slab = ROW_AXES, COLUMN_AXES
    in_specs = (
        P(dp, None, None, slab, None),
        P(dp, None, None, slab),
        P(dp, None, None, slab, None),
        P(),
        P(None, dp, slab),
        P(None, dp, slab),
        P(None, dp, slab),
        P(None, dp, slab),
    )
    out_specs = (
        P(None, dp, slab),
        P(None, dp, slab),
        P(None, dp, slab),
        P(None, dp, slab),
        P(None, None, slab),
    )
    return jax.shard_map(local, mesh=fine, in_specs=in_specs, out_specs=out_specs, check_vma=False)
```

```python
import jax
import jax.numpy as jnp
from jax import lax
from jax.sharding import PartitionSpec as P

C = 128
TAPS = 27
STEP_COUNT = 10


beta_first = 0.9
beta_second = 0.999
learning_rate = 0.01
weight_decay = 0.05
teacher_keep = 0.99
adam_epsilon = 1e-08


def with_halo(cells, sides, width):
    for axis, dim in sides:
        count = lax.axis_size(axis)
        ends = count - 1
        head = lax.slice_in_dim(cells, 0, width, axis=dim)
        tail = lax.slice_in_dim(cells, cells.shape[dim] - width, cells.shape[dim], axis=dim)
        cells = jnp.concatenate(
            [
                lax.ppermute(tail, axis, [(i, (i + 1) % count) for i in range(ends)]),
                cells,
                lax.ppermute(head, axis, [((i + 1) % count, i) for i in range(ends)]),
            ],
            axis=dim,
        )
    return cells


def tap_corners():
    return [
        (along_x, along_y, along_z)
        for along_x in range(3)
        for along_y in range(3)
        for along_z in range(3)
    ]


def unit_scale():
    return (TAPS * C) ** (-0.5)


def silu_slope(values):
    logistic = jax.nn.sigmoid(values)
    return logistic * (1.0 + values * (1.0 - logistic))


def take_window(padded, start, extent):
    window = padded[
        start[0] : start[0] + extent[0],
        start[1] : start[1] + extent[1],
        start[2] : start[2] + extent[2],
    ]
    return window.reshape(-1, window.shape[-1])


def stacked_windows(padded, starts, extent):
    return jnp.concatenate([take_window(padded, start, extent) for start in starts], axis=-1)


def forward_conv(padded, weight_rows, extent):
    channels = weight_rows.shape[1]
    columns = stacked_windows(padded, tap_corners(), extent)
    summed = jnp.dot(columns, weight_rows, preferred_element_type=jnp.float32)
    return (summed * unit_scale()).reshape(extent + (channels,))


def transposed_conv(padded_grad, weight_rows, extent):
    channels = weight_rows.shape[1]
    starts = [(2 - a, 2 - b, 2 - c) for a, b, c in tap_corners()]
    columns = stacked_windows(padded_grad, starts, extent)
    flipped = weight_rows.reshape(TAPS, channels, channels).transpose(0, 2, 1)
    summed = jnp.dot(
        columns, flipped.reshape(TAPS * channels, channels), preferred_element_type=jnp.float32
    )
    return (summed * unit_scale()).reshape(extent + (channels,))


def weight_grad(padded, grad_field, extent):
    grad_rows = grad_field.reshape(-1, grad_field.shape[-1])
    columns = stacked_windows(padded, tap_corners(), extent)
    return lax.dot_general(
        columns, grad_rows, (((0,), (0,)), ((), ())), preferred_element_type=jnp.float32
    )


def adam_update(master, moment, second, teacher, gradient):
    new_moment = beta_first * moment + (1.0 - beta_first) * gradient
    new_second = beta_second * second + (1.0 - beta_second) * gradient * gradient
    first_fix = 1.0 - beta_first**STEP_COUNT
    second_fix = 1.0 - beta_second**STEP_COUNT
    ratio = new_moment / first_fix / (jnp.sqrt(new_second / second_fix) + adam_epsilon)
    new_master = master - learning_rate * (ratio + weight_decay * master)
    new_teacher = teacher_keep * teacher + (1.0 - teacher_keep) * new_master
    return (new_master, new_moment, new_second, new_teacher)


def local(voxels, occupancy, out_grad, weights, master, moment, second, teacher):
    own_cells = voxels[0]
    extent = tuple(own_cells.shape[:3])
    occupied = occupancy[0].astype(jnp.float32)[..., None]
    plane_pad = ((1, 1), (1, 1), (0, 0), (0, 0))
    rim_input = with_halo(own_cells, ((COLUMN_AXES, 2),), 1)
    padded_in = jnp.pad(rim_input, plane_pad)
    pre_one = forward_conv(padded_in, weights[0], extent)
    act_one = (occupied * jax.nn.silu(pre_one)).astype(jnp.bfloat16)
    rim_hidden = with_halo(act_one, ((COLUMN_AXES, 2),), 1)
    padded_act = jnp.pad(rim_hidden, plane_pad)
    pre_two = forward_conv(padded_act, weights[1], extent)
    grad_two = (out_grad[0].astype(jnp.float32) * occupied * silu_slope(pre_two)).astype(
        jnp.bfloat16
    )
    rim_grad = with_halo(grad_two, ((COLUMN_AXES, 2),), 1)
    padded_grad = jnp.pad(rim_grad, plane_pad)
    cols = master.shape[-1]
    scene_in = whole_scene(own_cells)
    scene_act = whole_scene(act_one)
    scene_extent = tuple(scene_in.shape[:3])
    wgrad_two = weight_grad(pad_scene(scene_act), own_columns(grad_two, cols), scene_extent)
    back_one = transposed_conv(padded_grad, weights[1], extent)
    grad_one = (back_one * occupied * silu_slope(pre_one)).astype(jnp.bfloat16)
    wgrad_one = weight_grad(pad_scene(scene_in), own_columns(grad_one, cols), scene_extent)
    weight_grads = jnp.stack([wgrad_one, wgrad_two])
    gradient = scatter_rows_and_columns(weight_grads, master.shape)
    new_master, new_moment, new_second, new_teacher = adam_update(
        master, moment, second, teacher, gradient
    )
    fresh_weights = new_master.astype(jnp.bfloat16)
    new_weights = gather_rows(fresh_weights)
    return (new_master, new_moment, new_second, new_teacher, new_weights)


ROW_AXES = ("z", "x_lo", "core")
COLUMN_AXES = ("y", "x_hi")


def exchange_and_sum(blocks, axes):
    moved = lax.all_to_all(blocks, axes, 0, 0, tiled=True)
    return moved.sum(axis=0)


def whole_scene(cells):
    parts = 1
    for name in COLUMN_AXES:
        parts *= lax.axis_size(name)
    copies = jnp.broadcast_to(cells[None], (parts,) + cells.shape)
    return lax.all_to_all(copies, COLUMN_AXES, 0, 3, tiled=True)[0]


def pad_scene(cells):
    return jnp.pad(cells, ((1, 1), (1, 1), (1, 1), (0, 0)))


def own_columns(field, cols):
    split = field.reshape(field.shape[:3] + (field.shape[3] // cols, cols))
    moved = lax.all_to_all(split, COLUMN_AXES, 3, 2, tiled=True)
    return moved.reshape(moved.shape[:3] + (cols,))


def scatter_rows_and_columns(weight_grads, own_shape):
    layers, rows, cols = own_shape
    z, x_lo, core = (lax.axis_size(name) for name in ROW_AXES)
    blocks = weight_grads.reshape(layers, z, x_lo, core, rows, cols)
    blocks = blocks.transpose(3, 2, 1, 0, 4, 5).reshape(core, x_lo, z, layers, rows * cols)
    blocks = exchange_and_sum(blocks, "core")
    blocks = exchange_and_sum(blocks, "x_lo")
    blocks = exchange_and_sum(blocks, "z")
    return blocks.reshape(own_shape) * unit_scale()


def gather_rows(fresh_weights):
    layers, rows, cols = fresh_weights.shape
    gathered = lax.all_gather(fresh_weights, "z", axis=0)
    gathered = lax.all_gather(gathered, ("x_lo", "core"), axis=0)
    gathered = gathered.reshape((-1,) + gathered.shape[1:])
    x_lo, core = lax.axis_size("x_lo"), lax.axis_size("core")
    gathered = gathered.reshape((x_lo, core) + gathered.shape[1:])
    gathered = gathered.transpose(3, 2, 0, 1, 4, 5)
    return gathered.reshape(layers, -1, cols)


def solution(mesh):
    rows_over, columns_over = mesh.shape["dp"], mesh.shape["slab"]
    fine = jax.sharding.Mesh(
        mesh.devices.reshape(rows_over // 4, 2, 2, columns_over // 2, 2), ROW_AXES + COLUMN_AXES
    )
    dp, slab = ROW_AXES, COLUMN_AXES
    in_specs = (
        P(dp, None, None, slab, None),
        P(dp, None, None, slab),
        P(dp, None, None, slab, None),
        P(),
        P(None, dp, slab),
        P(None, dp, slab),
        P(None, dp, slab),
        P(None, dp, slab),
    )
    out_specs = (
        P(None, dp, slab),
        P(None, dp, slab),
        P(None, dp, slab),
        P(None, dp, slab),
        P(None, None, slab),
    )
    return jax.shard_map(local, mesh=fine, in_specs=in_specs, out_specs=out_specs, check_vma=False)
```

```python
import jax
import jax.numpy as jnp
from jax import lax
from jax.sharding import PartitionSpec as P

C = 128
TAPS = 27
STEP_COUNT = 10


beta_first = 0.9
beta_second = 0.999
learning_rate = 0.01
weight_decay = 0.05
teacher_keep = 0.99
adam_epsilon = 1e-08


def with_halo(cells, sides, width):
    for axis, dim in sides:
        count = lax.axis_size(axis)
        ends = count - 1
        head = lax.slice_in_dim(cells, 0, width, axis=dim)
        tail = lax.slice_in_dim(cells, cells.shape[dim] - width, cells.shape[dim], axis=dim)
        cells = jnp.concatenate(
            [
                lax.ppermute(tail, axis, [(i, (i + 1) % count) for i in range(ends)]),
                cells,
                lax.ppermute(head, axis, [((i + 1) % count, i) for i in range(ends)]),
            ],
            axis=dim,
        )
    return cells


def tap_corners():
    return [
        (along_x, along_y, along_z)
        for along_x in range(3)
        for along_y in range(3)
        for along_z in range(3)
    ]


def unit_scale():
    return (TAPS * C) ** (-0.5)


def silu_slope(values):
    logistic = jax.nn.sigmoid(values)
    return logistic * (1.0 + values * (1.0 - logistic))


def take_window(padded, start, extent):
    window = padded[
        start[0] : start[0] + extent[0],
        start[1] : start[1] + extent[1],
        start[2] : start[2] + extent[2],
    ]
    return window.reshape(-1, window.shape[-1])


def stacked_windows(padded, starts, extent):
    return jnp.concatenate([take_window(padded, start, extent) for start in starts], axis=-1)


def volume_conv(padded, kernel):
    summed = lax.conv_general_dilated(
        padded[None],
        kernel,
        (1, 1, 1),
        "VALID",
        dimension_numbers=("NDHWC", "DHWIO", "NDHWC"),
        preferred_element_type=jnp.float32,
    )
    return summed[0] * unit_scale()


def forward_conv(padded, weight_rows, extent):
    channels = weight_rows.shape[1]
    return volume_conv(padded, weight_rows.reshape(3, 3, 3, channels, channels))


def transposed_conv(padded_grad, weight_rows, extent):
    channels = weight_rows.shape[1]
    kernel = weight_rows.reshape(3, 3, 3, channels, channels)[::-1, ::-1, ::-1]
    return volume_conv(padded_grad, kernel.transpose(0, 1, 2, 4, 3))


def weight_grad(padded, grad_field, extent):
    grad_rows = grad_field.reshape(-1, grad_field.shape[-1])
    columns = stacked_windows(padded, tap_corners(), extent)
    return lax.dot_general(
        columns, grad_rows, (((0,), (0,)), ((), ())), preferred_element_type=jnp.float32
    )


def adam_update(master, moment, second, teacher, gradient):
    new_moment = beta_first * moment + (1.0 - beta_first) * gradient
    new_second = beta_second * second + (1.0 - beta_second) * gradient * gradient
    first_fix = 1.0 - beta_first**STEP_COUNT
    second_fix = 1.0 - beta_second**STEP_COUNT
    ratio = new_moment / first_fix / (jnp.sqrt(new_second / second_fix) + adam_epsilon)
    new_master = master - learning_rate * (ratio + weight_decay * master)
    new_teacher = teacher_keep * teacher + (1.0 - teacher_keep) * new_master
    return (new_master, new_moment, new_second, new_teacher)


def local(voxels, occupancy, out_grad, weights, master, moment, second, teacher):
    own_cells = voxels[0]
    extent = tuple(own_cells.shape[:3])
    occupied = occupancy[0].astype(jnp.float32)[..., None]
    plane_pad = ((1, 1), (1, 1), (0, 0), (0, 0))
    rim_input = with_halo(own_cells, ((COLUMN_AXES, 2),), 1)
    padded_in = jnp.pad(rim_input, plane_pad)
    pre_one = forward_conv(padded_in, weights[0], extent)
    act_one = (occupied * jax.nn.silu(pre_one)).astype(jnp.bfloat16)
    rim_hidden = with_halo(act_one, ((COLUMN_AXES, 2),), 1)
    padded_act = jnp.pad(rim_hidden, plane_pad)
    pre_two = forward_conv(padded_act, weights[1], extent)
    grad_two = (out_grad[0].astype(jnp.float32) * occupied * silu_slope(pre_two)).astype(
        jnp.bfloat16
    )
    rim_grad = with_halo(grad_two, ((COLUMN_AXES, 2),), 1)
    padded_grad = jnp.pad(rim_grad, plane_pad)
    wgrad_two = weight_grad(padded_act, grad_two, extent)
    back_one = transposed_conv(padded_grad, weights[1], extent)
    grad_one = (back_one * occupied * silu_slope(pre_one)).astype(jnp.bfloat16)
    wgrad_one = weight_grad(padded_in, grad_one, extent)
    weight_grads = jnp.stack([wgrad_one, wgrad_two])
    gradient = scatter_rows_and_columns(weight_grads, master.shape)
    new_master, new_moment, new_second, new_teacher = adam_update(
        master, moment, second, teacher, gradient
    )
    fresh_weights = new_master.astype(jnp.bfloat16)
    new_weights = gather_rows(fresh_weights)
    return (new_master, new_moment, new_second, new_teacher, new_weights)


ROW_AXES = ("z", "x_lo", "core")
COLUMN_AXES = ("y", "x_hi")


def exchange_and_sum(blocks, axes):
    moved = lax.all_to_all(blocks, axes, 0, 0, tiled=True)
    return moved.sum(axis=0)


def scatter_rows_and_columns(weight_grads, own_shape):
    layers, rows, cols = own_shape
    lanes = weight_grads.shape[-1]
    z, x_lo, core = (lax.axis_size(name) for name in ROW_AXES)
    y, x_hi = (lax.axis_size(name) for name in COLUMN_AXES)
    blocks = weight_grads.reshape(layers, z, x_lo, core, rows, lanes)
    blocks = blocks.transpose(3, 2, 1, 0, 4, 5)
    blocks = exchange_and_sum(blocks, "core")
    blocks = exchange_and_sum(blocks, "x_lo")
    blocks = exchange_and_sum(blocks, "z")
    blocks = blocks.reshape(layers, rows, y * x_hi, cols).transpose(2, 0, 1, 3)
    blocks = exchange_and_sum(blocks, COLUMN_AXES)
    return blocks * unit_scale()


def gather_rows(fresh_weights):
    layers, rows, cols = fresh_weights.shape
    gathered = lax.all_gather(fresh_weights, "z", axis=0)
    gathered = lax.all_gather(gathered, ("x_lo", "core"), axis=0)
    gathered = gathered.reshape((-1,) + gathered.shape[1:])
    x_lo, core = lax.axis_size("x_lo"), lax.axis_size("core")
    gathered = gathered.reshape((x_lo, core) + gathered.shape[1:])
    gathered = gathered.transpose(3, 2, 0, 1, 4, 5)
    return gathered.reshape(layers, -1, cols)


def solution(mesh):
    rows_over, columns_over = mesh.shape["dp"], mesh.shape["slab"]
    fine = jax.sharding.Mesh(
        mesh.devices.reshape(rows_over // 4, 2, 2, columns_over // 2, 2), ROW_AXES + COLUMN_AXES
    )
    dp, slab = ROW_AXES, COLUMN_AXES
    in_specs = (
        P(dp, None, None, slab, None),
        P(dp, None, None, slab),
        P(dp, None, None, slab, None),
        P(),
        P(None, dp, slab),
        P(None, dp, slab),
        P(None, dp, slab),
        P(None, dp, slab),
    )
    out_specs = (
        P(None, dp, slab),
        P(None, dp, slab),
        P(None, dp, slab),
        P(None, dp, slab),
        P(None, None, slab),
    )
    return jax.shard_map(local, mesh=fine, in_specs=in_specs, out_specs=out_specs, check_vma=False)
```

```python
import jax
import jax.numpy as jnp
from jax import lax
from jax.sharding import PartitionSpec as P

C = 128
TAPS = 27
STEP_COUNT = 10


beta_first = 0.9
beta_second = 0.999
learning_rate = 0.01
weight_decay = 0.05
teacher_keep = 0.99
adam_epsilon = 1e-08


def with_halo(cells, sides, width):
    for axis, dim in sides:
        count = lax.axis_size(axis)
        ends = count - 1
        head = lax.slice_in_dim(cells, 0, width, axis=dim)
        tail = lax.slice_in_dim(cells, cells.shape[dim] - width, cells.shape[dim], axis=dim)
        cells = jnp.concatenate(
            [
                lax.ppermute(tail, axis, [(i, (i + 1) % count) for i in range(ends)]),
                cells,
                lax.ppermute(head, axis, [((i + 1) % count, i) for i in range(ends)]),
            ],
            axis=dim,
        )
    return cells


def tap_corners():
    return [
        (along_x, along_y, along_z)
        for along_x in range(3)
        for along_y in range(3)
        for along_z in range(3)
    ]


def unit_scale():
    return (TAPS * C) ** (-0.5)


def silu_slope(values):
    logistic = jax.nn.sigmoid(values)
    return logistic * (1.0 + values * (1.0 - logistic))


def take_window(padded, start, extent):
    window = padded[
        start[0] : start[0] + extent[0],
        start[1] : start[1] + extent[1],
        start[2] : start[2] + extent[2],
    ]
    return window.reshape(-1, window.shape[-1])


def stacked_windows(padded, starts, extent):
    return jnp.concatenate([take_window(padded, start, extent) for start in starts], axis=-1)


def volume_conv(padded, kernel):
    summed = lax.conv_general_dilated(
        padded[None],
        kernel,
        (1, 1, 1),
        "VALID",
        dimension_numbers=("NDHWC", "DHWIO", "NDHWC"),
        preferred_element_type=jnp.float32,
    )
    return summed[0] * unit_scale()


def forward_conv(padded, weight_rows, extent):
    channels = weight_rows.shape[1]
    return volume_conv(padded, weight_rows.reshape(3, 3, 3, channels, channels))


def transposed_conv(padded_grad, weight_rows, extent):
    channels = weight_rows.shape[1]
    kernel = weight_rows.reshape(3, 3, 3, channels, channels)[::-1, ::-1, ::-1]
    return volume_conv(padded_grad, kernel.transpose(0, 1, 2, 4, 3))


def weight_grad(padded, grad_field, extent):
    grad_rows = grad_field.reshape(-1, grad_field.shape[-1])
    columns = stacked_windows(padded, tap_corners(), extent)
    return lax.dot_general(
        columns, grad_rows, (((0,), (0,)), ((), ())), preferred_element_type=jnp.float32
    )


def adam_update(master, moment, second, teacher, gradient):
    new_moment = beta_first * moment + (1.0 - beta_first) * gradient
    new_second = beta_second * second + (1.0 - beta_second) * gradient * gradient
    first_fix = 1.0 - beta_first**STEP_COUNT
    second_fix = 1.0 - beta_second**STEP_COUNT
    ratio = new_moment / first_fix / (jnp.sqrt(new_second / second_fix) + adam_epsilon)
    new_master = master - learning_rate * (ratio + weight_decay * master)
    new_teacher = teacher_keep * teacher + (1.0 - teacher_keep) * new_master
    return (new_master, new_moment, new_second, new_teacher)


def local(voxels, occupancy, out_grad, weights, master, moment, second, teacher):
    own_cells = voxels[0]
    extent = tuple(own_cells.shape[:3])
    occupied = occupancy[0].astype(jnp.float32)[..., None]
    plane_pad = ((1, 1), (1, 1), (0, 0), (0, 0))
    rim_input = with_halo(own_cells, ((COLUMN_AXES, 2),), 1)
    padded_in = jnp.pad(rim_input, plane_pad)
    pre_one = forward_conv(padded_in, weights[0], extent)
    act_one = (occupied * jax.nn.silu(pre_one)).astype(jnp.bfloat16)
    rim_hidden = with_halo(act_one, ((COLUMN_AXES, 2),), 1)
    padded_act = jnp.pad(rim_hidden, plane_pad)
    pre_two = forward_conv(padded_act, weights[1], extent)
    grad_two = (out_grad[0].astype(jnp.float32) * occupied * silu_slope(pre_two)).astype(
        jnp.bfloat16
    )
    rim_grad = with_halo(grad_two, ((COLUMN_AXES, 2),), 1)
    padded_grad = jnp.pad(rim_grad, plane_pad)
    wgrad_two = first_row_stages(weight_grad(padded_act, grad_two, extent), master.shape[1])
    back_one = transposed_conv(padded_grad, weights[1], extent)
    grad_one = (back_one * occupied * silu_slope(pre_one)).astype(jnp.bfloat16)
    wgrad_one = first_row_stages(weight_grad(padded_in, grad_one, extent), master.shape[1])
    weight_grads = jnp.stack([wgrad_one, wgrad_two], axis=1)
    gradient = scatter_rows_and_columns(weight_grads, master.shape)
    new_master, new_moment, new_second, new_teacher = adam_update(
        master, moment, second, teacher, gradient
    )
    fresh_weights = new_master.astype(jnp.bfloat16)
    new_weights = gather_rows(fresh_weights)
    return (new_master, new_moment, new_second, new_teacher, new_weights)


ROW_AXES = ("z", "x_lo", "core")
COLUMN_AXES = ("y", "x_hi")


def exchange_and_sum(blocks, axes):
    moved = lax.all_to_all(blocks, axes, 0, 0, tiled=True)
    return moved.sum(axis=0)


def first_row_stages(weight_rows, rows):
    lanes = weight_rows.shape[-1]
    z, x_lo, core = (lax.axis_size(name) for name in ROW_AXES)
    blocks = weight_rows.reshape(z, x_lo, core, rows, lanes).transpose(2, 1, 0, 3, 4)
    blocks = exchange_and_sum(blocks, "core")
    return exchange_and_sum(blocks, "x_lo")


def scatter_rows_and_columns(weight_grads, own_shape):
    layers, rows, cols = own_shape
    y, x_hi = (lax.axis_size(name) for name in COLUMN_AXES)
    blocks = exchange_and_sum(weight_grads, "z")
    blocks = blocks.reshape(layers, rows, y * x_hi, cols).transpose(2, 0, 1, 3)
    blocks = exchange_and_sum(blocks, COLUMN_AXES)
    return blocks * unit_scale()


def gather_rows(fresh_weights):
    layers, rows, cols = fresh_weights.shape
    gathered = lax.all_gather(fresh_weights, "z", axis=0)
    gathered = lax.all_gather(gathered, ("x_lo", "core"), axis=0)
    gathered = gathered.reshape((-1,) + gathered.shape[1:])
    x_lo, core = lax.axis_size("x_lo"), lax.axis_size("core")
    gathered = gathered.reshape((x_lo, core) + gathered.shape[1:])
    gathered = gathered.transpose(3, 2, 0, 1, 4, 5)
    return gathered.reshape(layers, -1, cols)


def solution(mesh):
    rows_over, columns_over = mesh.shape["dp"], mesh.shape["slab"]
    fine = jax.sharding.Mesh(
        mesh.devices.reshape(rows_over // 4, 2, 2, columns_over // 2, 2), ROW_AXES + COLUMN_AXES
    )
    dp, slab = ROW_AXES, COLUMN_AXES
    in_specs = (
        P(dp, None, None, slab, None),
        P(dp, None, None, slab),
        P(dp, None, None, slab, None),
        P(),
        P(None, dp, slab),
        P(None, dp, slab),
        P(None, dp, slab),
        P(None, dp, slab),
    )
    out_specs = (
        P(None, dp, slab),
        P(None, dp, slab),
        P(None, dp, slab),
        P(None, dp, slab),
        P(None, None, slab),
    )
    return jax.shard_map(local, mesh=fine, in_specs=in_specs, out_specs=out_specs, check_vma=False)
```

```python
import jax
import jax.numpy as jnp
from jax import lax
from jax.sharding import PartitionSpec as P

C = 128
TAPS = 27
STEP_COUNT = 10


beta_first = 0.9
beta_second = 0.999
learning_rate = 0.01
weight_decay = 0.05
teacher_keep = 0.99
adam_epsilon = 1e-08


def with_halo(cells, sides, width):
    for axis, dim in sides:
        count = lax.axis_size(axis)
        ends = count - 1
        head = lax.slice_in_dim(cells, 0, width, axis=dim)
        tail = lax.slice_in_dim(cells, cells.shape[dim] - width, cells.shape[dim], axis=dim)
        cells = jnp.concatenate(
            [
                lax.ppermute(tail, axis, [(i, (i + 1) % count) for i in range(ends)]),
                cells,
                lax.ppermute(head, axis, [((i + 1) % count, i) for i in range(ends)]),
            ],
            axis=dim,
        )
    return cells


def tap_corners():
    return [
        (along_x, along_y, along_z)
        for along_x in range(3)
        for along_y in range(3)
        for along_z in range(3)
    ]


def unit_scale():
    return (TAPS * C) ** (-0.5)


def silu_slope(values):
    logistic = jax.nn.sigmoid(values)
    return logistic * (1.0 + values * (1.0 - logistic))


def take_window(padded, start, extent):
    window = padded[
        start[0] : start[0] + extent[0],
        start[1] : start[1] + extent[1],
        start[2] : start[2] + extent[2],
    ]
    return window.reshape(-1, window.shape[-1])


def stacked_windows(padded, starts, extent):
    return jnp.concatenate([take_window(padded, start, extent) for start in starts], axis=-1)


def volume_conv(padded, kernel):
    summed = lax.conv_general_dilated(
        padded[None],
        kernel,
        (1, 1, 1),
        "VALID",
        dimension_numbers=("NDHWC", "DHWIO", "NDHWC"),
        preferred_element_type=jnp.float32,
    )
    return summed[0] * unit_scale()


def forward_conv(padded, weight_rows, extent):
    channels = weight_rows.shape[1]
    return volume_conv(padded, weight_rows.reshape(3, 3, 3, channels, channels))


def transposed_conv(padded_grad, weight_rows, extent):
    channels = weight_rows.shape[1]
    kernel = weight_rows.reshape(3, 3, 3, channels, channels)[::-1, ::-1, ::-1]
    return volume_conv(padded_grad, kernel.transpose(0, 1, 2, 4, 3))


def weight_grad(padded, grad_field, extent):
    grad_rows = grad_field.reshape(-1, grad_field.shape[-1])
    columns = stacked_windows(padded, tap_corners(), extent)
    return lax.dot_general(
        columns, grad_rows, (((0,), (0,)), ((), ())), preferred_element_type=jnp.float32
    )


def adam_update(master, moment, second, teacher, gradient):
    new_moment = beta_first * moment + (1.0 - beta_first) * gradient
    new_second = beta_second * second + (1.0 - beta_second) * gradient * gradient
    first_fix = 1.0 - beta_first**STEP_COUNT
    second_fix = 1.0 - beta_second**STEP_COUNT
    ratio = new_moment / first_fix / (jnp.sqrt(new_second / second_fix) + adam_epsilon)
    new_master = master - learning_rate * (ratio + weight_decay * master)
    new_teacher = teacher_keep * teacher + (1.0 - teacher_keep) * new_master
    return (new_master, new_moment, new_second, new_teacher)


def local(voxels, occupancy, out_grad, weights, master, moment, second, teacher):
    own_cells = voxels[0]
    extent = tuple(own_cells.shape[:3])
    occupied = occupancy[0].astype(jnp.float32)[..., None]
    plane_pad = ((1, 1), (1, 1), (0, 0), (0, 0))
    rim_input = with_halo(own_cells, ((COLUMN_AXES, 2),), 1)
    padded_in = jnp.pad(rim_input, plane_pad)
    pre_one = forward_conv(padded_in, weights[0], extent)
    act_one = (occupied * jax.nn.silu(pre_one)).astype(jnp.bfloat16)
    rim_hidden = with_halo(act_one, ((COLUMN_AXES, 2),), 1)
    padded_act = jnp.pad(rim_hidden, plane_pad)
    pre_two = forward_conv(padded_act, weights[1], extent)
    grad_two = (out_grad[0].astype(jnp.float32) * occupied * silu_slope(pre_two)).astype(
        jnp.bfloat16
    )
    rim_grad = with_halo(grad_two, ((COLUMN_AXES, 2),), 1)
    padded_grad = jnp.pad(rim_grad, plane_pad)
    wgrad_two = weight_grad(padded_act, grad_two, extent)
    back_one = transposed_conv(padded_grad, weights[1], extent)
    grad_one = (back_one * occupied * silu_slope(pre_one)).astype(jnp.bfloat16)
    wgrad_one = weight_grad(padded_in, grad_one, extent)
    weight_grads = jnp.stack([wgrad_one, wgrad_two])
    gradient = scatter_rows_and_columns(weight_grads, master.shape)
    new_master, new_moment, new_second, new_teacher = adam_update(
        master, moment, second, teacher, gradient
    )
    fresh_weights = new_master.astype(jnp.bfloat16)
    new_weights = gather_rows(fresh_weights)
    return (new_master, new_moment, new_second, new_teacher, new_weights)


ROW_AXES = ("z_hi", "z_lo", "x_lo", "core")
COLUMN_AXES = ("y", "x_hi")


def exchange_and_sum(blocks, axes):
    moved = lax.all_to_all(blocks, axes, 0, 0, tiled=True)
    return moved.sum(axis=0)


def scatter_rows_and_columns(weight_grads, own_shape):
    layers, rows, cols = own_shape
    lanes = weight_grads.shape[-1]
    z_hi, z_lo, x_lo, core = (lax.axis_size(name) for name in ROW_AXES)
    y, x_hi = (lax.axis_size(name) for name in COLUMN_AXES)
    blocks = weight_grads.reshape(layers, z_hi, z_lo, x_lo, core, rows, lanes)
    blocks = blocks.transpose(4, 3, 2, 1, 0, 5, 6)
    blocks = exchange_and_sum(blocks, "core")
    blocks = exchange_and_sum(blocks, "x_lo")
    blocks = exchange_and_sum(blocks, "z_lo")
    blocks = exchange_and_sum(blocks, "z_hi")
    blocks = blocks.reshape(layers, rows, y * x_hi, cols).transpose(2, 0, 1, 3)
    blocks = exchange_and_sum(blocks, COLUMN_AXES)
    return blocks * unit_scale()


def gather_rows(fresh_weights):
    layers, rows, cols = fresh_weights.shape
    gathered = lax.all_gather(fresh_weights, ("z_hi", "z_lo"), axis=0)
    gathered = lax.all_gather(gathered, ("x_lo", "core"), axis=0)
    gathered = gathered.reshape((-1,) + gathered.shape[1:])
    x_lo, core = lax.axis_size("x_lo"), lax.axis_size("core")
    gathered = gathered.reshape((x_lo, core) + gathered.shape[1:])
    gathered = gathered.transpose(3, 2, 0, 1, 4, 5)
    return gathered.reshape(layers, -1, cols)


def solution(mesh):
    rows_over, columns_over = mesh.shape["dp"], mesh.shape["slab"]
    fine = jax.sharding.Mesh(
        mesh.devices.reshape(rows_over // 16, 4, 2, 2, columns_over // 2, 2), ROW_AXES + COLUMN_AXES
    )
    dp, slab = ROW_AXES, COLUMN_AXES
    in_specs = (
        P(dp, None, None, slab, None),
        P(dp, None, None, slab),
        P(dp, None, None, slab, None),
        P(),
        P(None, dp, slab),
        P(None, dp, slab),
        P(None, dp, slab),
        P(None, dp, slab),
    )
    out_specs = (
        P(None, dp, slab),
        P(None, dp, slab),
        P(None, dp, slab),
        P(None, dp, slab),
        P(None, None, slab),
    )
    return jax.shard_map(local, mesh=fine, in_specs=in_specs, out_specs=out_specs, check_vma=False)
```

```python
import jax
import jax.numpy as jnp
from jax import lax
from jax.sharding import PartitionSpec as P

C = 128
TAPS = 27
STEP_COUNT = 10


beta_first = 0.9
beta_second = 0.999
learning_rate = 0.01
weight_decay = 0.05
teacher_keep = 0.99
adam_epsilon = 1e-08


def with_halo(cells, sides, width):
    for axis, dim in sides:
        count = lax.axis_size(axis)
        ends = count - 1
        head = lax.slice_in_dim(cells, 0, width, axis=dim)
        tail = lax.slice_in_dim(cells, cells.shape[dim] - width, cells.shape[dim], axis=dim)
        cells = jnp.concatenate(
            [
                lax.ppermute(tail, axis, [(i, (i + 1) % count) for i in range(ends)]),
                cells,
                lax.ppermute(head, axis, [((i + 1) % count, i) for i in range(ends)]),
            ],
            axis=dim,
        )
    return cells


def tap_corners():
    return [
        (along_x, along_y, along_z)
        for along_x in range(3)
        for along_y in range(3)
        for along_z in range(3)
    ]


def unit_scale():
    return (TAPS * C) ** (-0.5)


def silu_slope(values):
    logistic = jax.nn.sigmoid(values)
    return logistic * (1.0 + values * (1.0 - logistic))


def take_window(padded, start, extent):
    window = padded[
        start[0] : start[0] + extent[0],
        start[1] : start[1] + extent[1],
        start[2] : start[2] + extent[2],
    ]
    return window.reshape(-1, window.shape[-1])


def stacked_windows(padded, starts, extent):
    return jnp.concatenate([take_window(padded, start, extent) for start in starts], axis=-1)


def volume_conv(padded, kernel):
    summed = lax.conv_general_dilated(
        padded[None],
        kernel,
        (1, 1, 1),
        "VALID",
        dimension_numbers=("NDHWC", "DHWIO", "NDHWC"),
        preferred_element_type=jnp.float32,
    )
    return summed[0] * unit_scale()


def forward_conv(padded, weight_rows, extent):
    channels = weight_rows.shape[1]
    return volume_conv(padded, weight_rows.reshape(3, 3, 3, channels, channels))


def transposed_conv(padded_grad, weight_rows, extent):
    channels = weight_rows.shape[1]
    kernel = weight_rows.reshape(3, 3, 3, channels, channels)[::-1, ::-1, ::-1]
    return volume_conv(padded_grad, kernel.transpose(0, 1, 2, 4, 3))


def weight_grad(padded, grad_field, extent):
    grad_rows = grad_field.reshape(-1, grad_field.shape[-1])
    columns = stacked_windows(padded, tap_corners(), extent)
    return lax.dot_general(
        columns, grad_rows, (((0,), (0,)), ((), ())), preferred_element_type=jnp.float32
    )


def adam_update(master, moment, second, teacher, gradient):
    new_moment = beta_first * moment + (1.0 - beta_first) * gradient
    new_second = beta_second * second + (1.0 - beta_second) * gradient * gradient
    first_fix = 1.0 - beta_first**STEP_COUNT
    second_fix = 1.0 - beta_second**STEP_COUNT
    ratio = new_moment / first_fix / (jnp.sqrt(new_second / second_fix) + adam_epsilon)
    new_master = master - learning_rate * (ratio + weight_decay * master)
    new_teacher = teacher_keep * teacher + (1.0 - teacher_keep) * new_master
    return (new_master, new_moment, new_second, new_teacher)


def local(voxels, occupancy, out_grad, weights, master, moment, second, teacher):
    own_cells = voxels[0]
    extent = tuple(own_cells.shape[:3])
    occupied = occupancy[0].astype(jnp.float32)[..., None]
    plane_pad = ((1, 1), (1, 1), (0, 0), (0, 0))
    rim_input = with_halo(own_cells, ((COLUMN_AXES, 2),), 1)
    padded_in = jnp.pad(rim_input, plane_pad)
    pre_one = forward_conv(padded_in, weights[0], extent)
    act_one = (occupied * jax.nn.silu(pre_one)).astype(jnp.bfloat16)
    rim_hidden = with_halo(act_one, ((COLUMN_AXES, 2),), 1)
    padded_act = jnp.pad(rim_hidden, plane_pad)
    pre_two = forward_conv(padded_act, weights[1], extent)
    grad_two = (out_grad[0].astype(jnp.float32) * occupied * silu_slope(pre_two)).astype(
        jnp.bfloat16
    )
    rim_grad = with_halo(grad_two, ((COLUMN_AXES, 2),), 1)
    padded_grad = jnp.pad(rim_grad, plane_pad)
    wgrad_two = weight_grad(padded_act, grad_two, extent)
    back_one = transposed_conv(padded_grad, weights[1], extent)
    grad_one = (back_one * occupied * silu_slope(pre_one)).astype(jnp.bfloat16)
    wgrad_one = weight_grad(padded_in, grad_one, extent)
    weight_grads = jnp.stack([wgrad_one, wgrad_two])
    gradient = scatter_rows_and_columns(weight_grads, master.shape)
    new_master, new_moment, new_second, new_teacher = adam_update(
        master, moment, second, teacher, gradient
    )
    fresh_weights = new_master.astype(jnp.bfloat16)
    new_weights = gather_rows(fresh_weights)
    return (new_master, new_moment, new_second, new_teacher, new_weights)


ROW_AXES = ("z_hi", "z_lo", "x_lo", "core")
COLUMN_AXES = ("y", "x_hi")


def exchange_and_sum(blocks, axes):
    moved = lax.all_to_all(blocks, axes, 0, 0, tiled=True)
    return moved.sum(axis=0)


def scatter_rows_and_columns(weight_grads, own_shape):
    layers, rows, cols = own_shape
    lanes = weight_grads.shape[-1]
    z_hi, z_lo, x_lo, core = (lax.axis_size(name) for name in ROW_AXES)
    y, x_hi = (lax.axis_size(name) for name in COLUMN_AXES)
    blocks = weight_grads.reshape(layers, z_hi, z_lo, x_lo, core, rows, lanes)
    blocks = blocks.transpose(4, 3, 2, 1, 0, 5, 6)
    blocks = exchange_and_sum(blocks, "core")
    blocks = exchange_and_sum(blocks, "x_lo")
    blocks = exchange_and_sum(blocks, "z_lo")
    blocks = blocks.reshape(z_hi, layers, rows, y * x_hi, cols).transpose(0, 3, 1, 2, 4)
    blocks = blocks.reshape((z_hi * y * x_hi,) + blocks.shape[2:])
    blocks = exchange_and_sum(blocks, ("z_hi",) + COLUMN_AXES)
    return blocks * unit_scale()


def gather_rows(fresh_weights):
    layers, rows, cols = fresh_weights.shape
    gathered = lax.all_gather(fresh_weights, ("z_hi", "z_lo"), axis=0)
    gathered = lax.all_gather(gathered, ("x_lo", "core"), axis=0)
    gathered = gathered.reshape((-1,) + gathered.shape[1:])
    x_lo, core = lax.axis_size("x_lo"), lax.axis_size("core")
    gathered = gathered.reshape((x_lo, core) + gathered.shape[1:])
    gathered = gathered.transpose(3, 2, 0, 1, 4, 5)
    return gathered.reshape(layers, -1, cols)


def solution(mesh):
    rows_over, columns_over = mesh.shape["dp"], mesh.shape["slab"]
    fine = jax.sharding.Mesh(
        mesh.devices.reshape(rows_over // 16, 4, 2, 2, columns_over // 2, 2), ROW_AXES + COLUMN_AXES
    )
    dp, slab = ROW_AXES, COLUMN_AXES
    in_specs = (
        P(dp, None, None, slab, None),
        P(dp, None, None, slab),
        P(dp, None, None, slab, None),
        P(),
        P(None, dp, slab),
        P(None, dp, slab),
        P(None, dp, slab),
        P(None, dp, slab),
    )
    out_specs = (
        P(None, dp, slab),
        P(None, dp, slab),
        P(None, dp, slab),
        P(None, dp, slab),
        P(None, None, slab),
    )
    return jax.shard_map(local, mesh=fine, in_specs=in_specs, out_specs=out_specs, check_vma=False)
```

```python
import jax
import jax.numpy as jnp
from jax import lax
from jax.sharding import PartitionSpec as P

C = 128
TAPS = 27
STEP_COUNT = 10


beta_first = 0.9
beta_second = 0.999
learning_rate = 0.01
weight_decay = 0.05
teacher_keep = 0.99
adam_epsilon = 1e-08


def with_halo(cells, sides, width):
    for axis, dim in sides:
        count = lax.axis_size(axis)
        ends = count - 1
        head = lax.slice_in_dim(cells, 0, width, axis=dim)
        tail = lax.slice_in_dim(cells, cells.shape[dim] - width, cells.shape[dim], axis=dim)
        cells = jnp.concatenate(
            [
                lax.ppermute(tail, axis, [(i, (i + 1) % count) for i in range(ends)]),
                cells,
                lax.ppermute(head, axis, [((i + 1) % count, i) for i in range(ends)]),
            ],
            axis=dim,
        )
    return cells


def tap_corners():
    return [
        (along_x, along_y, along_z)
        for along_x in range(3)
        for along_y in range(3)
        for along_z in range(3)
    ]


def unit_scale():
    return (TAPS * C) ** (-0.5)


def silu_slope(values):
    logistic = jax.nn.sigmoid(values)
    return logistic * (1.0 + values * (1.0 - logistic))


def take_window(padded, start, extent):
    window = padded[
        start[0] : start[0] + extent[0],
        start[1] : start[1] + extent[1],
        start[2] : start[2] + extent[2],
    ]
    return window.reshape(-1, window.shape[-1])


def stacked_windows(padded, starts, extent):
    return jnp.concatenate([take_window(padded, start, extent) for start in starts], axis=-1)


def volume_conv(padded, kernel):
    summed = lax.conv_general_dilated(
        padded[None],
        kernel,
        (1, 1, 1),
        "VALID",
        dimension_numbers=("NDHWC", "DHWIO", "NDHWC"),
        preferred_element_type=jnp.float32,
    )
    return summed[0] * unit_scale()


def forward_conv(padded, weight_rows, extent):
    channels = weight_rows.shape[1]
    return volume_conv(padded, weight_rows.reshape(3, 3, 3, channels, channels))


def transposed_conv(padded_grad, weight_rows, extent):
    channels = weight_rows.shape[1]
    kernel = weight_rows.reshape(3, 3, 3, channels, channels)[::-1, ::-1, ::-1]
    return volume_conv(padded_grad, kernel.transpose(0, 1, 2, 4, 3))


def weight_grad(padded, grad_field, extent):
    grad_rows = grad_field.reshape(-1, grad_field.shape[-1])
    columns = stacked_windows(padded, tap_corners(), extent)
    return lax.dot_general(
        columns, grad_rows, (((0,), (0,)), ((), ())), preferred_element_type=jnp.float32
    )


def adam_update(master, moment, second, teacher, gradient):
    new_moment = beta_first * moment + (1.0 - beta_first) * gradient
    new_second = beta_second * second + (1.0 - beta_second) * gradient * gradient
    first_fix = 1.0 - beta_first**STEP_COUNT
    second_fix = 1.0 - beta_second**STEP_COUNT
    ratio = new_moment / first_fix / (jnp.sqrt(new_second / second_fix) + adam_epsilon)
    new_master = master - learning_rate * (ratio + weight_decay * master)
    new_teacher = teacher_keep * teacher + (1.0 - teacher_keep) * new_master
    return (new_master, new_moment, new_second, new_teacher)


def local(voxels, occupancy, out_grad, weights, master, moment, second, teacher):
    own_cells = voxels[0]
    extent = tuple(own_cells.shape[:3])
    occupied = occupancy[0].astype(jnp.float32)[..., None]
    plane_pad = ((1, 1), (1, 1), (0, 0), (0, 0))
    rim_input = with_halo(own_cells, ((COLUMN_AXES, 2),), 1)
    padded_in = jnp.pad(rim_input, plane_pad)
    pre_one = forward_conv(padded_in, weights[0], extent)
    act_one = (occupied * jax.nn.silu(pre_one)).astype(jnp.bfloat16)
    rim_hidden = with_halo(act_one, ((COLUMN_AXES, 2),), 1)
    padded_act = jnp.pad(rim_hidden, plane_pad)
    pre_two = forward_conv(padded_act, weights[1], extent)
    grad_two = (out_grad[0].astype(jnp.float32) * occupied * silu_slope(pre_two)).astype(
        jnp.bfloat16
    )
    rim_grad = with_halo(grad_two, ((COLUMN_AXES, 2),), 1)
    padded_grad = jnp.pad(rim_grad, plane_pad)
    wgrad_two = weight_grad(padded_act, grad_two, extent)
    back_one = transposed_conv(padded_grad, weights[1], extent)
    grad_one = (back_one * occupied * silu_slope(pre_one)).astype(jnp.bfloat16)
    wgrad_one = weight_grad(padded_in, grad_one, extent)
    weight_grads = jnp.stack([wgrad_one, wgrad_two])
    gradient = scatter_rows_and_columns(weight_grads, master.shape)
    new_master, new_moment, new_second, new_teacher = adam_update(
        master, moment, second, teacher, gradient
    )
    fresh_weights = new_master.astype(jnp.bfloat16)
    new_weights = gather_rows(fresh_weights)
    return (new_master, new_moment, new_second, new_teacher, new_weights)


ROW_AXES = ("z_hi", "z_lo", "x_lo", "core")
COLUMN_AXES = ("y", "x_hi")


def exchange_and_sum(blocks, axes):
    moved = lax.all_to_all(blocks, axes, 0, 0, tiled=True)
    return moved.sum(axis=0)


def scatter_rows_and_columns(weight_grads, own_shape):
    layers, rows, cols = own_shape
    lanes = weight_grads.shape[-1]
    z_hi, z_lo, x_lo, core = (lax.axis_size(name) for name in ROW_AXES)
    y, x_hi = (lax.axis_size(name) for name in COLUMN_AXES)
    blocks = weight_grads.reshape(layers, z_hi, z_lo, x_lo, core, rows, lanes)
    blocks = blocks.transpose(4, 3, 2, 1, 0, 5, 6)
    blocks = exchange_and_sum(blocks, "core")
    blocks = blocks.reshape((x_lo * z_lo,) + blocks.shape[2:])
    blocks = exchange_and_sum(blocks, ("x_lo", "z_lo"))
    blocks = blocks.reshape(z_hi, layers, rows, y * x_hi, cols).transpose(0, 3, 1, 2, 4)
    blocks = blocks.reshape((z_hi * y * x_hi,) + blocks.shape[2:])
    blocks = exchange_and_sum(blocks, ("z_hi",) + COLUMN_AXES)
    return blocks * unit_scale()


def gather_rows(fresh_weights):
    layers, rows, cols = fresh_weights.shape
    gathered = lax.all_gather(fresh_weights, ("z_hi", "z_lo"), axis=0)
    gathered = lax.all_gather(gathered, ("x_lo", "core"), axis=0)
    gathered = gathered.reshape((-1,) + gathered.shape[1:])
    x_lo, core = lax.axis_size("x_lo"), lax.axis_size("core")
    gathered = gathered.reshape((x_lo, core) + gathered.shape[1:])
    gathered = gathered.transpose(3, 2, 0, 1, 4, 5)
    return gathered.reshape(layers, -1, cols)


def solution(mesh):
    rows_over, columns_over = mesh.shape["dp"], mesh.shape["slab"]
    fine = jax.sharding.Mesh(
        mesh.devices.reshape(rows_over // 16, 4, 2, 2, columns_over // 2, 2), ROW_AXES + COLUMN_AXES
    )
    dp, slab = ROW_AXES, COLUMN_AXES
    in_specs = (
        P(dp, None, None, slab, None),
        P(dp, None, None, slab),
        P(dp, None, None, slab, None),
        P(),
        P(None, dp, slab),
        P(None, dp, slab),
        P(None, dp, slab),
        P(None, dp, slab),
    )
    out_specs = (
        P(None, dp, slab),
        P(None, dp, slab),
        P(None, dp, slab),
        P(None, dp, slab),
        P(None, None, slab),
    )
    return jax.shard_map(local, mesh=fine, in_specs=in_specs, out_specs=out_specs, check_vma=False)
```

```python
import jax
import jax.numpy as jnp
from jax import lax
from jax.sharding import PartitionSpec as P

C = 128
TAPS = 27
STEP_COUNT = 10


beta_first = 0.9
beta_second = 0.999
learning_rate = 0.01
weight_decay = 0.05
teacher_keep = 0.99
adam_epsilon = 1e-08


def with_halo(cells, sides, width):
    for axis, dim in sides:
        count = lax.axis_size(axis)
        ends = count - 1
        head = lax.slice_in_dim(cells, 0, width, axis=dim)
        tail = lax.slice_in_dim(cells, cells.shape[dim] - width, cells.shape[dim], axis=dim)
        cells = jnp.concatenate(
            [
                lax.ppermute(tail, axis, [(i, (i + 1) % count) for i in range(ends)]),
                cells,
                lax.ppermute(head, axis, [((i + 1) % count, i) for i in range(ends)]),
            ],
            axis=dim,
        )
    return cells


def tap_corners():
    return [
        (along_x, along_y, along_z)
        for along_x in range(3)
        for along_y in range(3)
        for along_z in range(3)
    ]


def unit_scale():
    return (TAPS * C) ** (-0.5)


def silu_slope(values):
    logistic = jax.nn.sigmoid(values)
    return logistic * (1.0 + values * (1.0 - logistic))


def take_window(padded, start, extent):
    window = padded[
        start[0] : start[0] + extent[0],
        start[1] : start[1] + extent[1],
        start[2] : start[2] + extent[2],
    ]
    return window.reshape(-1, window.shape[-1])


def stacked_windows(padded, starts, extent):
    return jnp.concatenate([take_window(padded, start, extent) for start in starts], axis=-1)


def volume_conv(padded, kernel):
    summed = lax.conv_general_dilated(
        padded[None],
        kernel,
        (1, 1, 1),
        "VALID",
        dimension_numbers=("NDHWC", "DHWIO", "NDHWC"),
        preferred_element_type=jnp.float32,
    )
    return summed[0] * unit_scale()


def forward_conv(padded, weight_rows, extent):
    channels = weight_rows.shape[1]
    return volume_conv(padded, weight_rows.reshape(3, 3, 3, channels, channels))


def transposed_conv(padded_grad, weight_rows, extent):
    channels = weight_rows.shape[1]
    kernel = weight_rows.reshape(3, 3, 3, channels, channels)[::-1, ::-1, ::-1]
    return volume_conv(padded_grad, kernel.transpose(0, 1, 2, 4, 3))


def weight_grad(padded, grad_field, extent):
    grad_rows = grad_field.reshape(-1, grad_field.shape[-1])
    columns = stacked_windows(padded, tap_corners(), extent)
    return lax.dot_general(
        columns, grad_rows, (((0,), (0,)), ((), ())), preferred_element_type=jnp.float32
    )


def adam_update(master, moment, second, teacher, gradient):
    new_moment = beta_first * moment + (1.0 - beta_first) * gradient
    new_second = beta_second * second + (1.0 - beta_second) * gradient * gradient
    first_fix = 1.0 - beta_first**STEP_COUNT
    second_fix = 1.0 - beta_second**STEP_COUNT
    ratio = new_moment / first_fix / (jnp.sqrt(new_second / second_fix) + adam_epsilon)
    new_master = master - learning_rate * (ratio + weight_decay * master)
    new_teacher = teacher_keep * teacher + (1.0 - teacher_keep) * new_master
    return (new_master, new_moment, new_second, new_teacher)


def local(voxels, occupancy, out_grad, weights, master, moment, second, teacher):
    own_cells = voxels[0]
    extent = tuple(own_cells.shape[:3])
    occupied = occupancy[0].astype(jnp.float32)[..., None]
    plane_pad = ((1, 1), (1, 1), (0, 0), (0, 0))
    rim_input = with_halo(own_cells, ((COLUMN_AXES, 2),), 1)
    padded_in = jnp.pad(rim_input, plane_pad)
    pre_one = forward_conv(padded_in, weights[0], extent)
    act_one = (occupied * jax.nn.silu(pre_one)).astype(jnp.bfloat16)
    rim_hidden = with_halo(act_one, ((COLUMN_AXES, 2),), 1)
    padded_act = jnp.pad(rim_hidden, plane_pad)
    pre_two = forward_conv(padded_act, weights[1], extent)
    grad_two = (out_grad[0].astype(jnp.float32) * occupied * silu_slope(pre_two)).astype(
        jnp.bfloat16
    )
    rim_grad = with_halo(grad_two, ((COLUMN_AXES, 2),), 1)
    padded_grad = jnp.pad(rim_grad, plane_pad)
    wgrad_two = weight_grad(padded_act, grad_two, extent)
    back_one = transposed_conv(padded_grad, weights[1], extent)
    grad_one = (back_one * occupied * silu_slope(pre_one)).astype(jnp.bfloat16)
    wgrad_one = weight_grad(padded_in, grad_one, extent)
    weight_grads = jnp.stack([wgrad_one, wgrad_two])
    gradient = scatter_rows_and_columns(weight_grads, master.shape)
    new_master, new_moment, new_second, new_teacher = adam_update(
        master, moment, second, teacher, gradient
    )
    fresh_weights = new_master.astype(jnp.bfloat16)
    new_weights = gather_rows(fresh_weights)
    return (new_master, new_moment, new_second, new_teacher, new_weights)


ROW_AXES = ("z_hi", "z_lo", "x_lo", "core")
COLUMN_AXES = ("y", "x_hi")


def exchange_and_sum(blocks, axes):
    moved = lax.all_to_all(blocks, axes, 0, 0, tiled=True)
    return moved.sum(axis=0)


def scatter_rows_and_columns(weight_grads, own_shape):
    layers, rows, cols = own_shape
    lanes = weight_grads.shape[-1]
    z_hi, z_lo, x_lo, core = (lax.axis_size(name) for name in ROW_AXES)
    y, x_hi = (lax.axis_size(name) for name in COLUMN_AXES)
    blocks = weight_grads.reshape(layers, z_hi, z_lo, x_lo, core, rows, lanes)
    blocks = blocks.transpose(4, 3, 2, 1, 0, 5, 6)
    blocks = exchange_and_sum(blocks, "core")
    blocks = blocks.reshape((x_lo * z_lo,) + blocks.shape[2:])
    blocks = exchange_and_sum(blocks, ("x_lo", "z_lo"))
    blocks = blocks.reshape(z_hi, layers, rows, y * x_hi, cols).transpose(0, 3, 1, 2, 4)
    blocks = blocks.reshape((z_hi * y * x_hi,) + blocks.shape[2:])
    blocks = exchange_and_sum(blocks, ("z_hi",) + COLUMN_AXES)
    return blocks * unit_scale()


def gather_rows(fresh_weights):
    layers, rows, cols = fresh_weights.shape
    gathered = lax.all_gather(fresh_weights, "z_hi", axis=0)
    gathered = lax.all_gather(gathered, ("z_lo", "x_lo", "core"), axis=0)
    return gathered.transpose(2, 1, 0, 3, 4).reshape(layers, -1, cols)


def solution(mesh):
    rows_over, columns_over = mesh.shape["dp"], mesh.shape["slab"]
    fine = jax.sharding.Mesh(
        mesh.devices.reshape(rows_over // 16, 4, 2, 2, columns_over // 2, 2), ROW_AXES + COLUMN_AXES
    )
    dp, slab = ROW_AXES, COLUMN_AXES
    in_specs = (
        P(dp, None, None, slab, None),
        P(dp, None, None, slab),
        P(dp, None, None, slab, None),
        P(),
        P(None, dp, slab),
        P(None, dp, slab),
        P(None, dp, slab),
        P(None, dp, slab),
    )
    out_specs = (
        P(None, dp, slab),
        P(None, dp, slab),
        P(None, dp, slab),
        P(None, dp, slab),
        P(None, None, slab),
    )
    return jax.shard_map(local, mesh=fine, in_specs=in_specs, out_specs=out_specs, check_vma=False)
```

```python
import jax
import jax.numpy as jnp
from jax import lax
from jax.sharding import PartitionSpec as P

C = 128
TAPS = 27
STEP_COUNT = 10


beta_first = 0.9
beta_second = 0.999
learning_rate = 0.01
weight_decay = 0.05
teacher_keep = 0.99
adam_epsilon = 1e-08


def with_halo(cells, sides, width):
    for axis, dim in sides:
        count = lax.axis_size(axis)
        ends = count - 1
        head = lax.slice_in_dim(cells, 0, width, axis=dim)
        tail = lax.slice_in_dim(cells, cells.shape[dim] - width, cells.shape[dim], axis=dim)
        cells = jnp.concatenate(
            [
                lax.ppermute(tail, axis, [(i, (i + 1) % count) for i in range(ends)]),
                cells,
                lax.ppermute(head, axis, [((i + 1) % count, i) for i in range(ends)]),
            ],
            axis=dim,
        )
    return cells


def tap_corners():
    return [
        (along_x, along_y, along_z)
        for along_x in range(3)
        for along_y in range(3)
        for along_z in range(3)
    ]


def unit_scale():
    return (TAPS * C) ** (-0.5)


def silu_slope(values):
    logistic = jax.nn.sigmoid(values)
    return logistic * (1.0 + values * (1.0 - logistic))


def take_window(padded, start, extent):
    window = padded[
        start[0] : start[0] + extent[0],
        start[1] : start[1] + extent[1],
        start[2] : start[2] + extent[2],
    ]
    return window.reshape(-1, window.shape[-1])


def stacked_windows(padded, starts, extent):
    return jnp.concatenate([take_window(padded, start, extent) for start in starts], axis=-1)


def volume_conv(padded, kernel):
    summed = lax.conv_general_dilated(
        padded[None],
        kernel,
        (1, 1, 1),
        "VALID",
        dimension_numbers=("NDHWC", "DHWIO", "NDHWC"),
        preferred_element_type=jnp.float32,
    )
    return summed[0] * unit_scale()


def forward_conv(padded, weight_rows, extent):
    channels = weight_rows.shape[1]
    return volume_conv(padded, weight_rows.reshape(3, 3, 3, channels, channels))


def transposed_conv(padded_grad, weight_rows, extent):
    channels = weight_rows.shape[1]
    kernel = weight_rows.reshape(3, 3, 3, channels, channels)[::-1, ::-1, ::-1]
    return volume_conv(padded_grad, kernel.transpose(0, 1, 2, 4, 3))


def weight_grad(padded, grad_field, extent):
    grad_rows = grad_field.reshape(-1, grad_field.shape[-1])
    columns = stacked_windows(padded, tap_corners(), extent)
    return lax.dot_general(
        columns, grad_rows, (((0,), (0,)), ((), ())), preferred_element_type=jnp.float32
    )


def adam_update(master, moment, second, teacher, gradient):
    new_moment = beta_first * moment + (1.0 - beta_first) * gradient
    new_second = beta_second * second + (1.0 - beta_second) * gradient * gradient
    first_fix = 1.0 - beta_first**STEP_COUNT
    second_fix = 1.0 - beta_second**STEP_COUNT
    ratio = new_moment / first_fix / (jnp.sqrt(new_second / second_fix) + adam_epsilon)
    new_master = master - learning_rate * (ratio + weight_decay * master)
    new_teacher = teacher_keep * teacher + (1.0 - teacher_keep) * new_master
    return (new_master, new_moment, new_second, new_teacher)


def local(voxels, occupancy, out_grad, weights, master, moment, second, teacher):
    own_cells = voxels[0]
    extent = tuple(own_cells.shape[:3])
    occupied = occupancy[0].astype(jnp.float32)[..., None]
    plane_pad = ((1, 1), (1, 1), (0, 0), (0, 0))
    rim_input = with_halo(own_cells, ((COLUMN_AXES, 2),), 1)
    padded_in = jnp.pad(rim_input, plane_pad)
    pre_one = forward_conv(padded_in, weights[0], extent)
    act_one = (occupied * jax.nn.silu(pre_one)).astype(jnp.bfloat16)
    rim_hidden = with_halo(act_one, ((COLUMN_AXES, 2),), 1)
    padded_act = jnp.pad(rim_hidden, plane_pad)
    pre_two = forward_conv(padded_act, weights[1], extent)
    grad_two = (out_grad[0].astype(jnp.float32) * occupied * silu_slope(pre_two)).astype(
        jnp.bfloat16
    )
    rim_grad = with_halo(grad_two, ((COLUMN_AXES, 2),), 1)
    padded_grad = jnp.pad(rim_grad, plane_pad)
    wgrad_two = weight_grad(padded_act, grad_two, extent)
    back_one = transposed_conv(padded_grad, weights[1], extent)
    grad_one = (back_one * occupied * silu_slope(pre_one)).astype(jnp.bfloat16)
    wgrad_one = weight_grad(padded_in, grad_one, extent)
    weight_grads = jnp.stack([wgrad_one, wgrad_two])
    gradient = scatter_rows_and_columns(weight_grads, master.shape)
    new_master, new_moment, new_second, new_teacher = adam_update(
        master, moment, second, teacher, gradient
    )
    fresh_weights = new_master.astype(jnp.bfloat16)
    new_weights = gather_rows(fresh_weights)
    return (new_master, new_moment, new_second, new_teacher, new_weights)


ROW_AXES = ("z_hi", "z_lo", "x_lo", "core")
COLUMN_AXES = ("y", "x_hi")


def exchange_and_sum(blocks, axes):
    moved = lax.all_to_all(blocks, axes, 0, 0, tiled=True)
    return moved.sum(axis=0)


def scatter_rows_and_columns(weight_grads, own_shape):
    layers, rows, cols = own_shape
    lanes = weight_grads.shape[-1]
    z_hi, z_lo, x_lo, core = (lax.axis_size(name) for name in ROW_AXES)
    y, x_hi = (lax.axis_size(name) for name in COLUMN_AXES)
    blocks = weight_grads.reshape(layers, z_hi, z_lo, x_lo, core, rows, lanes)
    blocks = blocks.transpose(4, 3, 2, 1, 0, 5, 6)
    blocks = exchange_and_sum(blocks, "core")
    blocks = blocks.reshape((x_lo * z_lo,) + blocks.shape[2:])
    blocks = exchange_and_sum(blocks, ("x_lo", "z_lo"))
    blocks = blocks.reshape(z_hi, layers, rows, y * x_hi, cols).transpose(0, 3, 1, 2, 4)
    blocks = blocks.reshape((z_hi * y * x_hi,) + blocks.shape[2:])
    blocks = exchange_and_sum(blocks, ("z_hi",) + COLUMN_AXES)
    return blocks * unit_scale()


def gather_rows(fresh_weights):
    layers, rows, cols = fresh_weights.shape
    z_hi, z_lo, x_lo, core = (lax.axis_size(name) for name in ROW_AXES)
    gathered = lax.all_gather(fresh_weights, ("x_lo", "z_lo"), axis=0)
    gathered = lax.all_gather(gathered, ("z_hi", "core"), axis=0)
    gathered = gathered.reshape((z_hi, core, x_lo, z_lo) + fresh_weights.shape)
    return gathered.transpose(4, 0, 3, 2, 1, 5, 6).reshape(layers, -1, cols)


def solution(mesh):
    rows_over, columns_over = mesh.shape["dp"], mesh.shape["slab"]
    fine = jax.sharding.Mesh(
        mesh.devices.reshape(rows_over // 16, 4, 2, 2, columns_over // 2, 2), ROW_AXES + COLUMN_AXES
    )
    dp, slab = ROW_AXES, COLUMN_AXES
    in_specs = (
        P(dp, None, None, slab, None),
        P(dp, None, None, slab),
        P(dp, None, None, slab, None),
        P(),
        P(None, dp, slab),
        P(None, dp, slab),
        P(None, dp, slab),
        P(None, dp, slab),
    )
    out_specs = (
        P(None, dp, slab),
        P(None, dp, slab),
        P(None, dp, slab),
        P(None, dp, slab),
        P(None, None, slab),
    )
    return jax.shard_map(local, mesh=fine, in_specs=in_specs, out_specs=out_specs, check_vma=False)
```
